256 devices in a mesh: dp: 4 (over x), ctx: 64 (over z, y, core).
Axes of the slice: x: 4, y: 4, z: 8, core: 2. Of those that a mesh axis runs over, the one named last changes fastest.
Arguments:
- inputs: bfloat16 [4, 16384, 2304], P('dp', 'ctx'), may hold values from -16 to 16
- query: bfloat16 [4, 16384, 1024], P('dp', 'ctx'), may hold values from -110 to 110
- w_key: bfloat16 [2304, 512], P('dp'), may hold values from -0.125 to 0.125
- w_value: bfloat16 [2304, 512], P('dp'), may hold values from -0.125 to 0.125
- doc_lengths: int32 [4, 16], P('dp'), may hold values from 1 to 4096, 16384 in all within a row
- grad_out: bfloat16 [4, 16384, 1024], P('dp', 'ctx'), may hold values from -6 to 6
Outputs:
- attended: bfloat16 [4, 16384, 1024], P('dp', 'ctx')
- grad_query: bfloat16 [4, 16384, 1024], P('dp', 'ctx')
- grad_input: bfloat16 [4, 16384, 2304], P('dp', 'ctx')
- grad_wkey: bfloat16 [2304, 512], P('dp')
- grad_wvalue: bfloat16 [2304, 512], P('dp')
The draws below stay inside these ranges and needn't reach their ends.
All inputs are finite; a program needn't handle non-finite values.
Results may differ from the reference program's by a relative error of at most 0.025.
The reference program's roundings to bfloat16 on the way count: a program that leaves them out, or rounds other values in their place, can miss the bound.
Values may be sent and summed in bfloat16 or wider, within the bound.
No kernel may reach another device: no remote copies, remote signals or barrier semaphores. Data moves between devices by JAX's collectives and lax.ppermute only.
A program may use at most 128 MiB of HBM per device.

```python
import math
import jax
import jax.numpy as jnp
import numpy as np
from jax import lax

D = 2304
HQ = 4
HK = 2
HD = 256
WINDOW = 2048
DOCS = 16
TOK_DEV = 256
SEQS = 4
LEN = 16384


def draw_query(key, part):
    full_shape = (SEQS, LEN, HQ * HD)
    return jnp.clip(jax.random.normal(key, full_shape, jnp.float32), -6.0, 6.0).astype(jnp.bfloat16)


def with_spikes(array, stream_key, source, target, shards_of, factor):
    owner, partner = [(jnp.arange(array.shape[position]) // (array.shape[position] // shards_of)).reshape([-1 if axis == position else 1 for axis in range(array.ndim)]) for position in (source, target)]
    chosen = jax.random.permutation(stream_key, shards_of)[partner]
    strong = (owner == chosen) | (owner == (partner + shards_of // 2) % shards_of)
    return jnp.where(strong, factor * array, array)


def steps_of(key, extent, cuts, least, high):
    factor_of, own = 1.0, jax.random.fold_in(key, 6)
    for axis_at, blocks in cuts:
        draws = jnp.exp(jax.random.uniform(jax.random.fold_in(own, axis_at), (blocks,), jnp.float32, least / len(cuts), high / len(cuts)))
        factor_of = factor_of * jnp.repeat(draws, extent[axis_at] // blocks).reshape([-1 if axis == axis_at else 1 for axis in range(len(extent))])
    return factor_of


def profile(amount, total, limit, slope):
    portions = [(1 << 20) // math.isqrt(standing ** slope) + 1 for standing in range(2, amount + 1)]
    spare, holding = total - limit - (amount - 1), [1] * (amount - 1)
    while spare > 0:
        movable = [i for i in range(amount - 1) if holding[i] < limit]
        pool, left = sum([portions[i] for i in movable]), spare
        for i in movable:
            addition = min(limit - holding[i], max(1, left * portions[i] // pool), spare)
            holding[i] = holding[i] + addition
            spare = spare - addition
    return np.array([limit] + holding)


def ragged_sizes(stream_key, number_of, total, most, slope):
    if number_of == 2:
        one = jax.random.randint(stream_key, (), max(1, total - most), min(most, total - 1) + 1)
        return jnp.stack([one, total - one])
    tallies = jnp.asarray(profile(number_of, total, most, slope), jnp.int32)
    twos = (number_of - 1) // 2
    source_of, receiver = tallies[1:1 + 2 * twos:2], tallies[2:2 + 2 * twos:2]
    margin = jnp.minimum(source_of - 1, most - receiver)
    passed = jax.random.randint(jax.random.fold_in(stream_key, 1), (twos,), 0, 1 << 20) % (margin + 1)
    tallies = tallies.at[1:1 + 2 * twos:2].set(source_of - passed).at[2:2 + 2 * twos:2].set(receiver + passed)
    return tallies[jax.random.permutation(jax.random.fold_in(stream_key, 2), number_of)]


def noise(stream_key, shape, deviation, reach, pieces=(), kind=jnp.bfloat16):
    entries = jax.random.normal(stream_key, shape, jnp.float32) * deviation
    if len(pieces) > 0:
        entries = steps_of(stream_key, shape, pieces, -0.22, 0.18) * entries
    return jnp.clip(entries, min=-reach, max=reach).astype(kind)


def gaussian_with(key, extent, spread, bound, pieces, heavy, kind=jnp.bfloat16):
    array = spread * jax.random.normal(key, extent, jnp.float32)
    if pieces:
        array = array * steps_of(key, extent, pieces, -0.22, 0.18)
    return jnp.clip(with_spikes(array, jax.random.fold_in(key, 3), *heavy), -bound, bound).astype(kind)


def setup_inputs(seed: int = 0) -> dict:
    streams_of = jax.random.split(jax.random.key(seed), 7)
    return {
        "inputs": gaussian_with(streams_of[0], (SEQS, LEN, D), 1.0, 16.0, ((0, 4), (1, 64)), (1, 2, 64, 4.0)),
        "query": draw_query(jax.random.fold_in(streams_of[6], 71), 0),
        "w_key": noise(streams_of[2], (D, HK * HD), D ** -0.5, 0.125, ((0, 4),)),
        "w_value": noise(streams_of[3], (D, HK * HD), D ** -0.5, 0.125, ((0, 4),)),
        "doc_lengths": jax.vmap(lambda own: ragged_sizes(own, DOCS, LEN, LEN // 4, 2))(jax.random.split(streams_of[4], SEQS)).reshape((SEQS, DOCS)).astype(jnp.int32),
        "grad_out": noise(streams_of[5], (SEQS, LEN, HQ * HD), 1.0, 6.0, ((0, 4), (1, 64))),
    }


def segment_of(lengths, positions):
    doc_ends = jnp.cumsum(lengths, dtype=jnp.int32)
    return jnp.sum((doc_ends[None, :] <= positions[:, None]).astype(jnp.int32), axis=1, dtype=jnp.int32)


def band_mask(query_pos, query_seg, key_pos, key_seg):
    distance_gap = query_pos[:, None] - key_pos[None, :]
    inside = (distance_gap >= 0) & (distance_gap < WINDOW) & (key_pos[None, :] >= 0)
    return inside & (query_seg[:, None] == key_seg[None, :])


def rounded(value_in):
    return lax.optimization_barrier(value_in.astype(jnp.bfloat16)).astype(jnp.float32)


def attend_block(query_rows, kv_rows, upstream_rows, allowed):
    score_scale = HD ** -0.5
    per_group = HQ // HK
    kv_width = HK * HD
    tok_rows = query_rows.shape[0]
    span_rows = kv_rows.shape[0]
    query_heads = query_rows.astype(jnp.float32).reshape(tok_rows, HK, per_group, HD)
    key_heads = kv_rows[:, :kv_width].astype(jnp.float32).reshape(span_rows, HK, HD)
    value_heads = kv_rows[:, kv_width:].astype(jnp.float32).reshape(span_rows, HK, HD)
    upstream_heads = upstream_rows.astype(jnp.float32).reshape(tok_rows, HK, per_group, HD)
    scores = jnp.einsum('qkgd,tkd->kgqt', query_heads, key_heads) * score_scale
    scores = jnp.where(allowed[None, None], scores, -jnp.inf)
    highest = jnp.max(scores, axis=-1, keepdims=True)
    log_total = highest + jnp.log(jnp.sum(jnp.exp(scores - highest), axis=-1, keepdims=True))
    softmax = jnp.exp(scores - log_total)
    soft_half = rounded(softmax)
    mixed = rounded(jnp.einsum('kgqt,tkd->qkgd', soft_half, value_heads))
    delta_sum = jnp.transpose(jnp.sum(upstream_heads * mixed, axis=-1), (1, 2, 0))[..., None]
    prob_grad = jnp.einsum('qkgd,tkd->kgqt', upstream_heads, value_heads)
    score_grad = rounded(softmax * (prob_grad - delta_sum) * score_scale)
    query_grad = jnp.einsum('kgqt,tkd->qkgd', score_grad, key_heads)
    key_grad = jnp.einsum('kgqt,qkgd->tkd', score_grad, query_heads)
    value_grad = jnp.einsum('kgqt,qkgd->tkd', soft_half, upstream_heads)
    kv_grad = jnp.concatenate([key_grad.reshape(span_rows, kv_width), value_grad.reshape(span_rows, kv_width)], axis=1)
    return mixed.reshape(tok_rows, HQ * HD).astype(jnp.bfloat16), query_grad.reshape(tok_rows, HQ * HD).astype(jnp.bfloat16), kv_grad


def reference(inputs, query, w_key, w_value, doc_lengths, grad_out):
    tok_rows = TOK_DEV
    pad_rows = (WINDOW // TOK_DEV) * tok_rows
    span_rows = pad_rows + tok_rows
    kv_width = HK * HD

    def one_sequence(seq_item):
        tokens, queries, lengths, upstream = seq_item
        key_rows = jnp.dot(tokens, w_key, preferred_element_type=jnp.float32).astype(jnp.bfloat16)
        value_rows = jnp.dot(tokens, w_value, preferred_element_type=jnp.float32).astype(jnp.bfloat16)
        kv_pad = jnp.concatenate([jnp.zeros((pad_rows, 2 * kv_width), jnp.bfloat16), jnp.concatenate([key_rows, value_rows], axis=1)], axis=0)
        key_pos_all = jnp.arange(LEN + pad_rows, dtype=jnp.int32) - pad_rows
        key_seg_all = segment_of(lengths, key_pos_all)
        query_pos_all = jnp.arange(LEN, dtype=jnp.int32)
        query_seg_all = segment_of(lengths, query_pos_all)

        def block_step(running, block_num):
            row_start = (block_num * tok_rows).astype(jnp.int32)
            query_block = lax.dynamic_slice_in_dim(queries, row_start, tok_rows, 0)
            upstream_block = lax.dynamic_slice_in_dim(upstream, row_start, tok_rows, 0)
            kv_block = lax.dynamic_slice_in_dim(kv_pad, row_start, span_rows, 0)
            allowed = band_mask(lax.dynamic_slice_in_dim(query_pos_all, row_start, tok_rows, 0),
                                lax.dynamic_slice_in_dim(query_seg_all, row_start, tok_rows, 0),
                                lax.dynamic_slice_in_dim(key_pos_all, row_start, span_rows, 0),
                                lax.dynamic_slice_in_dim(key_seg_all, row_start, span_rows, 0))
            mixed, query_grad, kv_grad = attend_block(query_block, kv_block, upstream_block, allowed)
            current = lax.dynamic_slice_in_dim(running, row_start, span_rows, 0)
            running = lax.dynamic_update_slice_in_dim(running, current + kv_grad, row_start, 0)
            return running, (mixed, query_grad)

        kv_grads, (mixed_all, query_grads) = lax.scan(block_step, jnp.zeros((LEN + pad_rows, 2 * kv_width), jnp.float32), jnp.arange(LEN // tok_rows, dtype=jnp.int32))
        kv_half = kv_grads[pad_rows:].astype(jnp.bfloat16)
        grad_input = (jnp.dot(kv_half[:, :kv_width], w_key.T, preferred_element_type=jnp.float32)
                      + jnp.dot(kv_half[:, kv_width:], w_value.T, preferred_element_type=jnp.float32)).astype(jnp.bfloat16)
        weight_term = jnp.dot(tokens.T, kv_half, preferred_element_type=jnp.float32)
        return mixed_all.reshape(LEN, HQ * HD), query_grads.reshape(LEN, HQ * HD), grad_input, weight_term

    results = lax.map(one_sequence, (inputs, query, doc_lengths, grad_out))
    weight_grad = jnp.sum(results[3], axis=0).astype(jnp.bfloat16)
    return results[0], results[1], results[2], weight_grad[:, :kv_width], weight_grad[:, kv_width:]
```

```python
import jax
import jax.numpy as jnp
from jax import lax
from jax.sharding import PartitionSpec as P

D = 2304
HQ = 4
HK = 2
HD = 256
WINDOW = 2048


FLOOR = -1e30


def from_behind(value, axis, by):
    peers = lax.axis_size(axis)
    pairs = [(i, i + by) for i in range(peers) if 0 <= i + by < peers]
    return lax.ppermute(value, axis, pairs)


def segment_of(lengths, positions):
    doc_ends = jnp.cumsum(lengths, dtype=jnp.int32)
    return jnp.sum(
        (doc_ends[None, :] <= positions[:, None]).astype(jnp.int32), axis=1, dtype=jnp.int32
    )


def band_mask(query_pos, query_seg, key_pos, key_seg):
    distance_gap = query_pos[:, None] - key_pos[None, :]
    inside = (distance_gap >= 0) & (distance_gap < WINDOW) & (key_pos[None, :] >= 0)
    return inside & (query_seg[:, None] == key_seg[None, :])


def masked_scores(query_heads, key_rows, allowed):
    key_heads = key_rows.reshape(key_rows.shape[0], HK, HD)
    scores = jnp.einsum(
        "qkgd,tkd->kgqt", query_heads, key_heads, preferred_element_type=jnp.float32
    ) * HD ** (-0.5)
    return jnp.where(allowed[None, None], scores, -jnp.inf)


def score_stats(scores):
    highest = jnp.maximum(jnp.max(scores, axis=-1), FLOOR)
    summed = jnp.sum(jnp.exp(scores - highest[..., None]), axis=-1)
    return (highest, summed)


def softmax_of(scores, log_total):
    softmax = jnp.exp(scores - log_total[..., None])
    return (softmax, softmax.astype(jnp.bfloat16))


def values_of(soft_half, value_rows):
    value_heads = value_rows.reshape(value_rows.shape[0], HK, HD)
    return jnp.einsum("kgqt,tkd->qkgd", soft_half, value_heads, preferred_element_type=jnp.float32)


def row_delta(upstream_heads, mixed_half):
    products = upstream_heads.astype(jnp.float32) * mixed_half.astype(jnp.float32)
    return jnp.transpose(jnp.sum(products, axis=-1), (1, 2, 0))


def band_grads(softmax, soft_half, query_heads, upstream_heads, delta_sum, key_rows, value_rows):
    span_rows = key_rows.shape[0]
    key_heads = key_rows.reshape(span_rows, HK, HD)
    value_heads = value_rows.reshape(span_rows, HK, HD)
    prob_grad = jnp.einsum(
        "qkgd,tkd->kgqt", upstream_heads, value_heads, preferred_element_type=jnp.float32
    )
    score_grad = (softmax * (prob_grad - delta_sum[..., None]) * HD ** (-0.5)).astype(jnp.bfloat16)
    query_grad = jnp.einsum(
        "kgqt,tkd->qkgd", score_grad, key_heads, preferred_element_type=jnp.float32
    )
    key_grad = jnp.einsum(
        "kgqt,qkgd->tkd", score_grad, query_heads, preferred_element_type=jnp.float32
    )
    value_grad = jnp.einsum(
        "kgqt,qkgd->tkd", soft_half, upstream_heads, preferred_element_type=jnp.float32
    )
    kv_grad = jnp.concatenate(
        [key_grad.reshape(span_rows, HK * HD), value_grad.reshape(span_rows, HK * HD)], axis=1
    )
    return (query_grad, kv_grad)


def shards(inputs, query, w_key, w_value, doc_lengths, grad_out):
    tokens = inputs[0]
    queries = query[0]
    upstream = grad_out[0]
    lengths = doc_lengths[0]
    tok_rows = tokens.shape[0]
    distant = WINDOW // tok_rows
    per_group = HQ // HK
    kv_width = HK * HD
    key_full, value_full = (
        lax.all_gather(w_key, "dp", axis=0, tiled=True),
        lax.all_gather(w_value, "dp", axis=0, tiled=True),
    )
    key_own = jnp.dot(tokens, key_full, preferred_element_type=jnp.float32).astype(jnp.bfloat16)
    value_own = jnp.dot(tokens, value_full, preferred_element_type=jnp.float32).astype(jnp.bfloat16)
    kv_own = jnp.concatenate([key_own, value_own], axis=1)
    earlier = jnp.concatenate(
        [from_behind(kv_own, "ctx", distance) for distance in range(distant, 0, -1)], axis=0
    )
    window = jnp.concatenate([earlier, kv_own], axis=0)
    device_index = lax.axis_index("ctx")
    first_row = device_index * tok_rows
    query_pos = first_row + jnp.arange(tok_rows, dtype=jnp.int32)
    key_pos = first_row - distant * tok_rows + jnp.arange((distant + 1) * tok_rows, dtype=jnp.int32)
    allowed = band_mask(
        query_pos, segment_of(lengths, query_pos), key_pos, segment_of(lengths, key_pos)
    )
    query_heads = queries.reshape(tok_rows, HK, per_group, HD)
    upstream_heads = upstream.reshape(tok_rows, HK, per_group, HD)
    scores = masked_scores(query_heads, window[:, :kv_width], allowed)
    highest, summed = score_stats(scores)
    log_total = highest + jnp.log(summed)
    softmax, soft_half = softmax_of(scores, log_total)
    mixed_half = values_of(soft_half, window[:, kv_width:]).astype(jnp.bfloat16)
    delta_sum = row_delta(upstream_heads, mixed_half)
    query_grad, window_grad = band_grads(
        softmax,
        soft_half,
        query_heads,
        upstream_heads,
        delta_sum,
        window[:, :kv_width],
        window[:, kv_width:],
    )
    own_grad = window_grad[distant * tok_rows :]
    earlier_grad = window_grad[: distant * tok_rows]
    for distance in range(1, distant + 1):
        lower = (distant - distance) * tok_rows
        own_grad = own_grad + from_behind(
            earlier_grad[lower : lower + tok_rows].astype(jnp.bfloat16), "ctx", -distance
        ).astype(jnp.float32)
    kv_grad = own_grad.astype(jnp.bfloat16)
    grad_input = (
        jnp.dot(kv_grad[:, :kv_width], key_full.T, preferred_element_type=jnp.float32)
        + jnp.dot(kv_grad[:, kv_width:], value_full.T, preferred_element_type=jnp.float32)
    ).astype(jnp.bfloat16)
    dp_size = lax.axis_size("dp")
    ctx_size = lax.axis_size("ctx")
    row_share = D // dp_size
    col_share = 2 * kv_width // ctx_size
    weight_part = jnp.einsum(
        "tar,tcj->acrj",
        tokens.reshape(tok_rows, dp_size, row_share),
        kv_grad.reshape(tok_rows, ctx_size, col_share),
        preferred_element_type=jnp.float32,
    ).reshape(dp_size * ctx_size, row_share, col_share)
    share_sum = lax.psum_scatter(weight_part, ("dp", "ctx"), scatter_dimension=0, tiled=True)
    share_sum = lax.optimization_barrier(share_sum)
    gathered = lax.all_gather(share_sum.astype(jnp.bfloat16), "ctx", axis=0, tiled=True)
    weight_grad = jnp.transpose(gathered, (1, 0, 2)).reshape(row_share, 2 * kv_width)
    attended = mixed_half.reshape(1, tok_rows, HQ * HD)
    grad_query = query_grad.astype(jnp.bfloat16).reshape(1, tok_rows, HQ * HD)
    return (
        attended,
        grad_query,
        grad_input.reshape(1, tok_rows, D),
        weight_grad[:, :kv_width],
        weight_grad[:, kv_width:],
    )


def solution(mesh):
    in_specs = (
        P("dp", "ctx", None),
        P("dp", "ctx", None),
        P("dp", None),
        P("dp", None),
        P("dp", None),
        P("dp", "ctx", None),
    )
    out_specs = (
        P("dp", "ctx", None),
        P("dp", "ctx", None),
        P("dp", "ctx", None),
        P("dp", None),
        P("dp", None),
    )
    return jax.shard_map(shards, mesh=mesh, in_specs=in_specs, out_specs=out_specs, check_vma=False)
```

```python
import jax
import jax.numpy as jnp
from jax import lax
from jax.sharding import PartitionSpec as P

D = 2304
HQ = 4
HK = 2
HD = 256
WINDOW = 2048


FLOOR = -1e30
CTX = ("z", "y", "c")


def ctx_size():
    return lax.axis_size("z") * lax.axis_size("y") * lax.axis_size("c")


def from_behind(value, axis, by):
    peers = ctx_size()
    pairs = [(i, i + by) for i in range(peers) if 0 <= i + by < peers]
    return lax.ppermute(value, axis, pairs)


def segment_of(lengths, positions):
    doc_ends = jnp.cumsum(lengths, dtype=jnp.int32)
    return jnp.sum(
        (doc_ends[None, :] <= positions[:, None]).astype(jnp.int32), axis=1, dtype=jnp.int32
    )


def band_mask(query_pos, query_seg, key_pos, key_seg):
    distance_gap = query_pos[:, None] - key_pos[None, :]
    inside = (distance_gap >= 0) & (distance_gap < WINDOW) & (key_pos[None, :] >= 0)
    return inside & (query_seg[:, None] == key_seg[None, :])


def masked_scores(query_heads, key_rows, allowed):
    key_heads = key_rows.reshape(key_rows.shape[0], HK, HD)
    scores = jnp.einsum(
        "qkgd,tkd->kgqt", query_heads, key_heads, preferred_element_type=jnp.float32
    ) * HD ** (-0.5)
    return jnp.where(allowed[None, None], scores, -jnp.inf)


def score_stats(scores):
    highest = jnp.maximum(jnp.max(scores, axis=-1), FLOOR)
    summed = jnp.sum(jnp.exp(scores - highest[..., None]), axis=-1)
    return (highest, summed)


def softmax_of(scores, log_total):
    softmax = jnp.exp(scores - log_total[..., None])
    return (softmax, softmax.astype(jnp.bfloat16))


def values_of(soft_half, value_rows):
    value_heads = value_rows.reshape(value_rows.shape[0], HK, HD)
    return jnp.einsum("kgqt,tkd->qkgd", soft_half, value_heads, preferred_element_type=jnp.float32)


def row_delta(upstream_heads, mixed_half):
    products = upstream_heads.astype(jnp.float32) * mixed_half.astype(jnp.float32)
    return jnp.transpose(jnp.sum(products, axis=-1), (1, 2, 0))


def band_grads(softmax, soft_half, query_heads, upstream_heads, delta_sum, key_rows, value_rows):
    span_rows = key_rows.shape[0]
    key_heads = key_rows.reshape(span_rows, HK, HD)
    value_heads = value_rows.reshape(span_rows, HK, HD)
    prob_grad = jnp.einsum(
        "qkgd,tkd->kgqt", upstream_heads, value_heads, preferred_element_type=jnp.float32
    )
    score_grad = (softmax * (prob_grad - delta_sum[..., None]) * HD ** (-0.5)).astype(jnp.bfloat16)
    query_grad = jnp.einsum(
        "kgqt,tkd->qkgd", score_grad, key_heads, preferred_element_type=jnp.float32
    )
    key_grad = jnp.einsum(
        "kgqt,qkgd->tkd", score_grad, query_heads, preferred_element_type=jnp.float32
    )
    value_grad = jnp.einsum(
        "kgqt,qkgd->tkd", soft_half, upstream_heads, preferred_element_type=jnp.float32
    )
    kv_grad = jnp.concatenate(
        [key_grad.reshape(span_rows, HK * HD), value_grad.reshape(span_rows, HK * HD)], axis=1
    )
    return (query_grad, kv_grad)


def shards(inputs, query, w_key, w_value, doc_lengths, grad_out):
    tokens = inputs[0]
    queries = query[0]
    upstream = grad_out[0]
    lengths = doc_lengths[0]
    tok_rows = tokens.shape[0]
    distant = WINDOW // tok_rows
    per_group = HQ // HK
    kv_width = HK * HD
    core = lax.axis_index("c")
    mine = jnp.stack([w_key, w_value])[core]
    both = lax.all_gather(lax.all_gather(mine, "dp", axis=0, tiled=True), "c", axis=0)
    key_full, value_full = both[0], both[1]
    key_own = jnp.dot(tokens, key_full, preferred_element_type=jnp.float32).astype(jnp.bfloat16)
    value_own = jnp.dot(tokens, value_full, preferred_element_type=jnp.float32).astype(jnp.bfloat16)
    kv_own = jnp.concatenate([key_own, value_own], axis=1)
    earlier = jnp.concatenate(
        [from_behind(kv_own, CTX, distance) for distance in range(distant, 0, -1)], axis=0
    )
    window = jnp.concatenate([earlier, kv_own], axis=0)
    device_index = lax.axis_index(CTX)
    first_row = device_index * tok_rows
    query_pos = first_row + jnp.arange(tok_rows, dtype=jnp.int32)
    key_pos = first_row - distant * tok_rows + jnp.arange((distant + 1) * tok_rows, dtype=jnp.int32)
    allowed = band_mask(
        query_pos, segment_of(lengths, query_pos), key_pos, segment_of(lengths, key_pos)
    )
    query_heads = queries.reshape(tok_rows, HK, per_group, HD)
    upstream_heads = upstream.reshape(tok_rows, HK, per_group, HD)
    scores = masked_scores(query_heads, window[:, :kv_width], allowed)
    highest, summed = score_stats(scores)
    log_total = highest + jnp.log(summed)
    softmax, soft_half = softmax_of(scores, log_total)
    mixed_half = values_of(soft_half, window[:, kv_width:]).astype(jnp.bfloat16)
    delta_sum = row_delta(upstream_heads, mixed_half)
    query_grad, window_grad = band_grads(
        softmax,
        soft_half,
        query_heads,
        upstream_heads,
        delta_sum,
        window[:, :kv_width],
        window[:, kv_width:],
    )
    own_grad = window_grad[distant * tok_rows :]
    earlier_grad = window_grad[: distant * tok_rows]
    for distance in range(1, distant + 1):
        lower = (distant - distance) * tok_rows
        own_grad = own_grad + from_behind(
            earlier_grad[lower : lower + tok_rows].astype(jnp.bfloat16), CTX, -distance
        ).astype(jnp.float32)
    kv_grad = own_grad.astype(jnp.bfloat16)
    grad_input = (
        jnp.dot(kv_grad[:, :kv_width], key_full.T, preferred_element_type=jnp.float32)
        + jnp.dot(kv_grad[:, kv_width:], value_full.T, preferred_element_type=jnp.float32)
    ).astype(jnp.bfloat16)
    dp_size = lax.axis_size("dp")
    z_size, y_size, c_size = lax.axis_size("z"), lax.axis_size("y"), lax.axis_size("c")
    row_share = D // dp_size
    rows_z = row_share // z_size
    cols_cy = 2 * kv_width // (c_size * y_size)
    weight_part = jnp.einsum(
        "tazr,tcyj->cyazrj",
        tokens.reshape(tok_rows, dp_size, z_size, rows_z),
        kv_grad.reshape(tok_rows, c_size, y_size, cols_cy),
        preferred_element_type=jnp.float32,
    )
    part = lax.psum_scatter(weight_part, "c", scatter_dimension=0, tiled=True)[0]
    part = lax.psum_scatter(part, "y", scatter_dimension=0, tiled=True)[0]
    part = lax.psum_scatter(part, "dp", scatter_dimension=0, tiled=True)[0]
    part = lax.psum_scatter(part, "z", scatter_dimension=0, tiled=True)
    part = lax.optimization_barrier(part).astype(jnp.bfloat16)
    part = lax.all_gather(part, "z", axis=0, tiled=True).reshape(row_share, cols_cy)
    part = lax.all_gather(part, "y", axis=0)
    part = lax.all_gather(part, "c", axis=0)
    weight_grad = jnp.transpose(part, (2, 0, 1, 3)).reshape(row_share, 2 * kv_width)
    attended = mixed_half.reshape(1, tok_rows, HQ * HD)
    grad_query = query_grad.astype(jnp.bfloat16).reshape(1, tok_rows, HQ * HD)
    return (
        attended,
        grad_query,
        grad_input.reshape(1, tok_rows, D),
        weight_grad[:, :kv_width],
        weight_grad[:, kv_width:],
    )


def solution(mesh):
    z_size = mesh.devices.shape[1] // 8
    split = jax.sharding.Mesh(
        mesh.devices.reshape(mesh.devices.shape[0], z_size, 4, 2), ("dp",) + CTX
    )
    tokens_spec = P("dp", CTX, None)
    in_specs = (tokens_spec, tokens_spec, P("dp", None), P("dp", None), P("dp", None), tokens_spec)
    out_specs = (tokens_spec, tokens_spec, tokens_spec, P("dp", None), P("dp", None))
    return jax.shard_map(shards, mesh=split, in_specs=in_specs, out_specs=out_specs, check_vma=False)
```

```python
import jax
import jax.numpy as jnp
from jax import lax
from jax.sharding import PartitionSpec as P

D = 2304
HQ = 4
HK = 2
HD = 256
WINDOW = 2048


FLOOR = -1e30
CTX = ("z", "y", "c")


def ctx_size():
    return lax.axis_size("z") * lax.axis_size("y") * lax.axis_size("c")


def from_behind(value, axis, by):
    peers = ctx_size()
    pairs = [(i, i + by) for i in range(peers) if 0 <= i + by < peers]
    return lax.ppermute(value, axis, pairs)


def segment_of(lengths, positions):
    doc_ends = jnp.cumsum(lengths, dtype=jnp.int32)
    return jnp.sum(
        (doc_ends[None, :] <= positions[:, None]).astype(jnp.int32), axis=1, dtype=jnp.int32
    )


def band_mask(query_pos, query_seg, key_pos, key_seg):
    distance_gap = query_pos[:, None] - key_pos[None, :]
    inside = (distance_gap >= 0) & (distance_gap < WINDOW) & (key_pos[None, :] >= 0)
    return inside & (query_seg[:, None] == key_seg[None, :])


def masked_scores(query_heads, key_rows, allowed):
    key_heads = key_rows.reshape(key_rows.shape[0], HK, HD)
    scores = jnp.einsum(
        "qkgd,tkd->kgqt", query_heads, key_heads, preferred_element_type=jnp.float32
    ) * HD ** (-0.5)
    return jnp.where(allowed[None, None], scores, -jnp.inf)


def score_stats(scores):
    highest = jnp.maximum(jnp.max(scores, axis=-1), FLOOR)
    summed = jnp.sum(jnp.exp(scores - highest[..., None]), axis=-1)
    return (highest, summed)


def softmax_of(scores, log_total):
    softmax = jnp.exp(scores - log_total[..., None])
    return (softmax, softmax.astype(jnp.bfloat16))


def values_of(soft_half, value_rows):
    value_heads = value_rows.reshape(value_rows.shape[0], HK, HD)
    return jnp.einsum("kgqt,tkd->qkgd", soft_half, value_heads, preferred_element_type=jnp.float32)


def row_delta(upstream_heads, mixed_half):
    products = upstream_heads.astype(jnp.float32) * mixed_half.astype(jnp.float32)
    return jnp.transpose(jnp.sum(products, axis=-1), (1, 2, 0))


def band_grads(softmax, soft_half, query_heads, upstream_heads, delta_sum, key_rows, value_rows, block_rows):
    span_rows = key_rows.shape[0]
    key_heads = key_rows.reshape(span_rows, HK, HD)
    value_heads = value_rows.reshape(span_rows, HK, HD)
    prob_grad = jnp.einsum(
        "qkgd,tkd->kgqt", upstream_heads, value_heads, preferred_element_type=jnp.float32
    )
    score_grad = (softmax * (prob_grad - delta_sum[..., None]) * HD ** (-0.5)).astype(jnp.bfloat16)
    kv_blocks = []
    for block in range(span_rows // block_rows):
        cols = slice(block * block_rows, (block + 1) * block_rows)
        key_grad = jnp.einsum(
            "kgqt,qkgd->tkd", score_grad[..., cols], query_heads, preferred_element_type=jnp.float32
        )
        value_grad = jnp.einsum(
            "kgqt,qkgd->tkd", soft_half[..., cols], upstream_heads, preferred_element_type=jnp.float32
        )
        kv_blocks.append(
            jnp.concatenate(
                [key_grad.reshape(block_rows, HK * HD), value_grad.reshape(block_rows, HK * HD)], axis=1
            )
        )
    query_grad = jnp.einsum(
        "kgqt,tkd->qkgd", score_grad, key_heads, preferred_element_type=jnp.float32
    )
    return (query_grad, kv_blocks)


def shards(inputs, query, w_key, w_value, doc_lengths, grad_out):
    tokens = inputs[0]
    queries = query[0]
    upstream = grad_out[0]
    lengths = doc_lengths[0]
    tok_rows = tokens.shape[0]
    distant = WINDOW // tok_rows
    per_group = HQ // HK
    kv_width = HK * HD
    core = lax.axis_index("c")
    mine = jnp.stack([w_key, w_value])[core]
    both = lax.all_gather(lax.all_gather(mine, "dp", axis=0, tiled=True), "c", axis=0)
    key_full, value_full = both[0], both[1]
    key_own = jnp.dot(tokens, key_full, preferred_element_type=jnp.float32).astype(jnp.bfloat16)
    value_own = jnp.dot(tokens, value_full, preferred_element_type=jnp.float32).astype(jnp.bfloat16)
    kv_own = jnp.concatenate([key_own, value_own], axis=1)
    earlier = jnp.concatenate(
        [from_behind(kv_own, CTX, distance) for distance in range(distant, 0, -1)], axis=0
    )
    window = jnp.concatenate([earlier, kv_own], axis=0)
    device_index = lax.axis_index(CTX)
    first_row = device_index * tok_rows
    query_pos = first_row + jnp.arange(tok_rows, dtype=jnp.int32)
    key_pos = first_row - distant * tok_rows + jnp.arange((distant + 1) * tok_rows, dtype=jnp.int32)
    allowed = band_mask(
        query_pos, segment_of(lengths, query_pos), key_pos, segment_of(lengths, key_pos)
    )
    query_heads = queries.reshape(tok_rows, HK, per_group, HD)
    upstream_heads = upstream.reshape(tok_rows, HK, per_group, HD)
    scores = masked_scores(query_heads, window[:, :kv_width], allowed)
    highest, summed = score_stats(scores)
    log_total = highest + jnp.log(summed)
    softmax, soft_half = softmax_of(scores, log_total)
    mixed_half = values_of(soft_half, window[:, kv_width:]).astype(jnp.bfloat16)
    delta_sum = row_delta(upstream_heads, mixed_half)
    query_grad, kv_blocks = band_grads(
        softmax,
        soft_half,
        query_heads,
        upstream_heads,
        delta_sum,
        window[:, :kv_width],
        window[:, kv_width:],
        tok_rows,
    )
    own_grad = kv_blocks[distant]
    for distance in range(distant, 0, -1):
        own_grad = own_grad + from_behind(
            kv_blocks[distant - distance].astype(jnp.bfloat16), CTX, -distance
        ).astype(jnp.float32)
    kv_grad = own_grad.astype(jnp.bfloat16)
    grad_input = (
        jnp.dot(kv_grad[:, :kv_width], key_full.T, preferred_element_type=jnp.float32)
        + jnp.dot(kv_grad[:, kv_width:], value_full.T, preferred_element_type=jnp.float32)
    ).astype(jnp.bfloat16)
    dp_size = lax.axis_size("dp")
    z_size, y_size, c_size = lax.axis_size("z"), lax.axis_size("y"), lax.axis_size("c")
    row_share = D // dp_size
    rows_z = row_share // z_size
    cols_cy = 2 * kv_width // (c_size * y_size)
    weight_part = jnp.einsum(
        "tazr,tcyj->cyazrj",
        tokens.reshape(tok_rows, dp_size, z_size, rows_z),
        kv_grad.reshape(tok_rows, c_size, y_size, cols_cy),
        preferred_element_type=jnp.float32,
    )
    part = lax.psum_scatter(weight_part.astype(jnp.bfloat16), "c", scatter_dimension=0, tiled=True)[0]
    part = lax.psum_scatter(part, "y", scatter_dimension=0, tiled=True)[0]
    part = lax.psum_scatter(part.astype(jnp.float32), "dp", scatter_dimension=0, tiled=True)[0]
    part = lax.psum_scatter(part, "z", scatter_dimension=0, tiled=True)
    part = lax.optimization_barrier(part).astype(jnp.bfloat16)
    part = lax.all_gather(part, "z", axis=0, tiled=True).reshape(row_share, cols_cy)
    part = lax.all_gather(part, "y", axis=0)
    part = lax.all_gather(part, "c", axis=0)
    weight_grad = jnp.transpose(part, (2, 0, 1, 3)).reshape(row_share, 2 * kv_width)
    attended = mixed_half.reshape(1, tok_rows, HQ * HD)
    grad_query = query_grad.astype(jnp.bfloat16).reshape(1, tok_rows, HQ * HD)
    return (
        attended,
        grad_query,
        grad_input.reshape(1, tok_rows, D),
        weight_grad[:, :kv_width],
        weight_grad[:, kv_width:],
    )


def solution(mesh):
    z_size = mesh.devices.shape[1] // 8
    split = jax.sharding.Mesh(
        mesh.devices.reshape(mesh.devices.shape[0], z_size, 4, 2), ("dp",) + CTX
    )
    tokens_spec = P("dp", CTX, None)
    in_specs = (tokens_spec, tokens_spec, P("dp", None), P("dp", None), P("dp", None), tokens_spec)
    out_specs = (tokens_spec, tokens_spec, tokens_spec, P("dp", None), P("dp", None))
    return jax.shard_map(shards, mesh=split, in_specs=in_specs, out_specs=out_specs, check_vma=False)
```

```python
import jax
import jax.numpy as jnp
from jax import lax
from jax.sharding import PartitionSpec as P

D = 2304
HQ = 4
HK = 2
HD = 256
WINDOW = 2048


FLOOR = -1e30
CTX = ("z", "y", "c")


def ctx_size():
    return lax.axis_size("z") * lax.axis_size("y") * lax.axis_size("c")


def from_behind(value, axis, by):
    peers = ctx_size()
    pairs = [(i, i + by) for i in range(peers) if 0 <= i + by < peers]
    return lax.ppermute(value, axis, pairs)


def segment_of(lengths, positions):
    doc_ends = jnp.cumsum(lengths, dtype=jnp.int32)
    return jnp.sum(
        (doc_ends[None, :] <= positions[:, None]).astype(jnp.int32), axis=1, dtype=jnp.int32
    )


def band_mask(query_pos, query_seg, key_pos, key_seg):
    distance_gap = query_pos[:, None] - key_pos[None, :]
    inside = (distance_gap >= 0) & (distance_gap < WINDOW) & (key_pos[None, :] >= 0)
    return inside & (query_seg[:, None] == key_seg[None, :])


def masked_scores(query_heads, key_rows, allowed):
    key_heads = key_rows.reshape(key_rows.shape[0], HK, HD)
    scores = jnp.einsum(
        "qkgd,tkd->kgqt", query_heads, key_heads, preferred_element_type=jnp.float32
    ) * HD ** (-0.5)
    return jnp.where(allowed[None, None], scores, -jnp.inf)


def score_stats(scores):
    highest = jnp.maximum(jnp.max(scores, axis=-1), FLOOR)
    summed = jnp.sum(jnp.exp(scores - highest[..., None]), axis=-1)
    return (highest, summed)


def softmax_of(scores, log_total):
    softmax = jnp.exp(scores - log_total[..., None])
    return (softmax, softmax.astype(jnp.bfloat16))


def values_of(soft_half, value_rows):
    value_heads = value_rows.reshape(value_rows.shape[0], HK, HD)
    return jnp.einsum("kgqt,tkd->qkgd", soft_half, value_heads, preferred_element_type=jnp.float32)


def row_delta(upstream_heads, mixed_half):
    products = upstream_heads.astype(jnp.float32) * mixed_half.astype(jnp.float32)
    return jnp.transpose(jnp.sum(products, axis=-1), (1, 2, 0))


def band_grads(softmax, soft_half, query_heads, upstream_heads, delta_sum, key_rows, value_rows, block_rows):
    span_rows = key_rows.shape[0]
    key_heads = key_rows.reshape(span_rows, HK, HD)
    value_heads = value_rows.reshape(span_rows, HK, HD)
    prob_grad = jnp.einsum(
        "qkgd,tkd->kgqt", upstream_heads, value_heads, preferred_element_type=jnp.float32
    )
    score_grad = (softmax * (prob_grad - delta_sum[..., None]) * HD ** (-0.5)).astype(jnp.bfloat16)
    kv_blocks = []
    for block in range(span_rows // block_rows):
        cols = slice(block * block_rows, (block + 1) * block_rows)
        key_grad = jnp.einsum(
            "kgqt,qkgd->tkd", score_grad[..., cols], query_heads, preferred_element_type=jnp.float32
        )
        value_grad = jnp.einsum(
            "kgqt,qkgd->tkd", soft_half[..., cols], upstream_heads, preferred_element_type=jnp.float32
        )
        kv_blocks.append(
            jnp.concatenate(
                [key_grad.reshape(block_rows, HK * HD), value_grad.reshape(block_rows, HK * HD)], axis=1
            )
        )
    query_grad = jnp.einsum(
        "kgqt,tkd->qkgd", score_grad, key_heads, preferred_element_type=jnp.float32
    )
    return (query_grad, kv_blocks)


def shards(inputs, query, w_key, w_value, doc_lengths, grad_out):
    tokens = inputs[0]
    queries = query[0]
    upstream = grad_out[0]
    lengths = doc_lengths[0]
    tok_rows = tokens.shape[0]
    distant = WINDOW // tok_rows
    per_group = HQ // HK
    kv_width = HK * HD
    core = lax.axis_index("c")
    dp_size = lax.axis_size("dp")
    dp_index = lax.axis_index("dp")
    mine = jnp.stack([w_key, w_value])[core]
    arrived = [mine] + [
        lax.ppermute(mine, "dp", [(i, (i + by) % dp_size) for i in range(dp_size)])
        for by in range(1, dp_size)
    ]
    order = (dp_index - jnp.arange(dp_size, dtype=jnp.int32)) % dp_size
    mine_full = jnp.take(jnp.stack(arrived), order, axis=0).reshape(D, kv_width)
    other_full = lax.ppermute(mine_full, "c", [(0, 1), (1, 0)])
    first = core == 0
    key_full = jnp.where(first, mine_full, other_full)
    value_full = jnp.where(first, other_full, mine_full)
    key_own = jnp.dot(tokens, key_full, preferred_element_type=jnp.float32).astype(jnp.bfloat16)
    value_own = jnp.dot(tokens, value_full, preferred_element_type=jnp.float32).astype(jnp.bfloat16)
    kv_own = jnp.concatenate([key_own, value_own], axis=1)
    earlier = jnp.concatenate(
        [from_behind(kv_own, CTX, distance) for distance in range(distant, 0, -1)], axis=0
    )
    window = jnp.concatenate([earlier, kv_own], axis=0)
    device_index = lax.axis_index(CTX)
    first_row = device_index * tok_rows
    query_pos = first_row + jnp.arange(tok_rows, dtype=jnp.int32)
    key_pos = first_row - distant * tok_rows + jnp.arange((distant + 1) * tok_rows, dtype=jnp.int32)
    allowed = band_mask(
        query_pos, segment_of(lengths, query_pos), key_pos, segment_of(lengths, key_pos)
    )
    query_heads = queries.reshape(tok_rows, HK, per_group, HD)
    upstream_heads = upstream.reshape(tok_rows, HK, per_group, HD)
    scores = masked_scores(query_heads, window[:, :kv_width], allowed)
    highest, summed = score_stats(scores)
    log_total = highest + jnp.log(summed)
    softmax, soft_half = softmax_of(scores, log_total)
    mixed_half = values_of(soft_half, window[:, kv_width:]).astype(jnp.bfloat16)
    delta_sum = row_delta(upstream_heads, mixed_half)
    query_grad, kv_blocks = band_grads(
        softmax,
        soft_half,
        query_heads,
        upstream_heads,
        delta_sum,
        window[:, :kv_width],
        window[:, kv_width:],
        tok_rows,
    )
    own_grad = kv_blocks[distant]
    for distance in range(distant, 0, -1):
        own_grad = own_grad + from_behind(
            kv_blocks[distant - distance].astype(jnp.bfloat16), CTX, -distance
        ).astype(jnp.float32)
    kv_grad = own_grad.astype(jnp.bfloat16)
    grad_input = (
        jnp.dot(kv_grad[:, :kv_width], key_full.T, preferred_element_type=jnp.float32)
        + jnp.dot(kv_grad[:, kv_width:], value_full.T, preferred_element_type=jnp.float32)
    ).astype(jnp.bfloat16)
    z_size, y_size, c_size = lax.axis_size("z"), lax.axis_size("y"), lax.axis_size("c")
    row_share = D // dp_size
    rows_z = row_share // z_size
    cols_cy = 2 * kv_width // (c_size * y_size)
    weight_part = jnp.einsum(
        "tazr,tcyj->cyazrj",
        tokens.reshape(tok_rows, dp_size, z_size, rows_z),
        kv_grad.reshape(tok_rows, c_size, y_size, cols_cy),
        preferred_element_type=jnp.float32,
    )
    partner = lax.ppermute(weight_part[1 - core].astype(jnp.bfloat16), "c", [(0, 1), (1, 0)])
    part = weight_part[core] + partner.astype(jnp.float32)
    part = lax.psum_scatter(part.astype(jnp.bfloat16), "y", scatter_dimension=0, tiled=True)[0]
    part = lax.psum_scatter(part.astype(jnp.float32), "dp", scatter_dimension=0, tiled=True)[0]
    part = lax.psum_scatter(part, "z", scatter_dimension=0, tiled=True)
    part = lax.optimization_barrier(part).astype(jnp.bfloat16)
    part = lax.all_gather(part, "z", axis=0, tiled=True).reshape(row_share, cols_cy)
    part = lax.all_gather(part, "y", axis=0)
    part = lax.all_gather(part, "c", axis=0)
    weight_grad = jnp.transpose(part, (2, 0, 1, 3)).reshape(row_share, 2 * kv_width)
    attended = mixed_half.reshape(1, tok_rows, HQ * HD)
    grad_query = query_grad.astype(jnp.bfloat16).reshape(1, tok_rows, HQ * HD)
    return (
        attended,
        grad_query,
        grad_input.reshape(1, tok_rows, D),
        weight_grad[:, :kv_width],
        weight_grad[:, kv_width:],
    )


def solution(mesh):
    z_size = mesh.devices.shape[1] // 8
    split = jax.sharding.Mesh(
        mesh.devices.reshape(mesh.devices.shape[0], z_size, 4, 2), ("dp",) + CTX
    )
    tokens_spec = P("dp", CTX, None)
    in_specs = (tokens_spec, tokens_spec, P("dp", None), P("dp", None), P("dp", None), tokens_spec)
    out_specs = (tokens_spec, tokens_spec, tokens_spec, P("dp", None), P("dp", None))
    return jax.shard_map(shards, mesh=split, in_specs=in_specs, out_specs=out_specs, check_vma=False)
```

```python
import jax
import jax.numpy as jnp
from jax import lax
from jax.sharding import PartitionSpec as P

D = 2304
HQ = 4
HK = 2
HD = 256
WINDOW = 2048


FLOOR = -1e30
CTX = ("z", "y", "c")


def ctx_size():
    return lax.axis_size("z") * lax.axis_size("y") * lax.axis_size("c")


def from_behind(value, axis, by):
    peers = ctx_size()
    pairs = [(i, i + by) for i in range(peers) if 0 <= i + by < peers]
    return lax.ppermute(value, axis, pairs)


def segment_of(lengths, positions):
    doc_ends = jnp.cumsum(lengths, dtype=jnp.int32)
    return jnp.sum(
        (doc_ends[None, :] <= positions[:, None]).astype(jnp.int32), axis=1, dtype=jnp.int32
    )


def band_mask(query_pos, query_seg, key_pos, key_seg):
    distance_gap = query_pos[:, None] - key_pos[None, :]
    inside = (distance_gap >= 0) & (distance_gap < WINDOW) & (key_pos[None, :] >= 0)
    return inside & (query_seg[:, None] == key_seg[None, :])


def masked_scores(query_heads, key_rows, allowed):
    key_heads = key_rows.reshape(key_rows.shape[0], HK, HD)
    scores = jnp.einsum(
        "qkgd,tkd->kgqt", query_heads, key_heads, preferred_element_type=jnp.float32
    ) * HD ** (-0.5)
    return jnp.where(allowed[None, None], scores, -jnp.inf)


def score_stats(scores):
    highest = jnp.maximum(jnp.max(scores, axis=-1), FLOOR)
    summed = jnp.sum(jnp.exp(scores - highest[..., None]), axis=-1)
    return (highest, summed)


def softmax_of(scores, log_total):
    softmax = jnp.exp(scores - log_total[..., None])
    return (softmax, softmax.astype(jnp.bfloat16))


def values_of(soft_half, value_rows):
    value_heads = value_rows.reshape(value_rows.shape[0], HK, HD)
    return jnp.einsum("kgqt,tkd->qkgd", soft_half, value_heads, preferred_element_type=jnp.float32)


def row_delta(upstream_heads, mixed_half):
    products = upstream_heads.astype(jnp.float32) * mixed_half.astype(jnp.float32)
    return jnp.transpose(jnp.sum(products, axis=-1), (1, 2, 0))


def band_grads(softmax, soft_half, query_heads, upstream_heads, delta_sum, key_rows, value_rows, block_rows):
    span_rows = key_rows.shape[0]
    key_heads = key_rows.reshape(span_rows, HK, HD)
    value_heads = value_rows.reshape(span_rows, HK, HD)
    prob_grad = jnp.einsum(
        "qkgd,tkd->kgqt", upstream_heads, value_heads, preferred_element_type=jnp.float32
    )
    score_grad = (softmax * (prob_grad - delta_sum[..., None]) * HD ** (-0.5)).astype(jnp.bfloat16)
    kv_blocks = []
    for block in range(span_rows // block_rows):
        cols = slice(block * block_rows, (block + 1) * block_rows)
        key_grad = jnp.einsum(
            "kgqt,qkgd->tkd", score_grad[..., cols], query_heads, preferred_element_type=jnp.float32
        )
        value_grad = jnp.einsum(
            "kgqt,qkgd->tkd", soft_half[..., cols], upstream_heads, preferred_element_type=jnp.float32
        )
        kv_blocks.append(
            jnp.concatenate(
                [key_grad.reshape(block_rows, HK * HD), value_grad.reshape(block_rows, HK * HD)], axis=1
            )
        )
    query_grad = jnp.einsum(
        "kgqt,tkd->qkgd", score_grad, key_heads, preferred_element_type=jnp.float32
    )
    return (query_grad, kv_blocks)


def shards(inputs, query, w_key, w_value, doc_lengths, grad_out):
    tokens = inputs[0]
    queries = query[0]
    upstream = grad_out[0]
    lengths = doc_lengths[0]
    tok_rows = tokens.shape[0]
    distant = WINDOW // tok_rows
    per_group = HQ // HK
    kv_width = HK * HD
    core = lax.axis_index("c")
    dp_size = lax.axis_size("dp")
    dp_index = lax.axis_index("dp")
    mine = jnp.stack([w_key, w_value])[core]
    arrived = [mine] + [
        lax.ppermute(mine, "dp", [(i, (i + by) % dp_size) for i in range(dp_size)])
        for by in range(1, dp_size)
    ]
    order = (dp_index - jnp.arange(dp_size, dtype=jnp.int32)) % dp_size
    mine_full = jnp.take(jnp.stack(arrived), order, axis=0).reshape(D, kv_width)
    other_full = lax.ppermute(mine_full, "c", [(0, 1), (1, 0)])
    first = core == 0
    key_full = jnp.where(first, mine_full, other_full)
    value_full = jnp.where(first, other_full, mine_full)
    key_own = jnp.dot(tokens, key_full, preferred_element_type=jnp.float32).astype(jnp.bfloat16)
    value_own = jnp.dot(tokens, value_full, preferred_element_type=jnp.float32).astype(jnp.bfloat16)
    kv_own = jnp.concatenate([key_own, value_own], axis=1)
    earlier = jnp.concatenate(
        [from_behind(kv_own, CTX, distance) for distance in range(distant, 0, -1)], axis=0
    )
    window = jnp.concatenate([earlier, kv_own], axis=0)
    device_index = lax.axis_index(CTX)
    first_row = device_index * tok_rows
    query_pos = first_row + jnp.arange(tok_rows, dtype=jnp.int32)
    key_pos = first_row - distant * tok_rows + jnp.arange((distant + 1) * tok_rows, dtype=jnp.int32)
    allowed = band_mask(
        query_pos, segment_of(lengths, query_pos), key_pos, segment_of(lengths, key_pos)
    )
    query_heads = queries.reshape(tok_rows, HK, per_group, HD)
    upstream_heads = upstream.reshape(tok_rows, HK, per_group, HD)
    scores = masked_scores(query_heads, window[:, :kv_width], allowed)
    highest, summed = score_stats(scores)
    log_total = highest + jnp.log(summed)
    softmax, soft_half = softmax_of(scores, log_total)
    mixed_half = values_of(soft_half, window[:, kv_width:]).astype(jnp.bfloat16)
    delta_sum = row_delta(upstream_heads, mixed_half)
    query_grad, kv_blocks = band_grads(
        softmax,
        soft_half,
        query_heads,
        upstream_heads,
        delta_sum,
        window[:, :kv_width],
        window[:, kv_width:],
        tok_rows,
    )
    own_grad = kv_blocks[distant]
    for distance in range(distant, 0, -1):
        own_grad = own_grad + from_behind(
            kv_blocks[distant - distance].astype(jnp.bfloat16), CTX, -distance
        ).astype(jnp.float32)
    kv_grad = own_grad.astype(jnp.bfloat16)
    grad_input = (
        jnp.dot(kv_grad[:, :kv_width], key_full.T, preferred_element_type=jnp.float32)
        + jnp.dot(kv_grad[:, kv_width:], value_full.T, preferred_element_type=jnp.float32)
    ).astype(jnp.bfloat16)
    z_size, y_size, c_size = lax.axis_size("z"), lax.axis_size("y"), lax.axis_size("c")
    row_share = D // dp_size
    rows_z = row_share // z_size
    cols_cy = 2 * kv_width // (c_size * y_size)
    weight_part = jnp.einsum(
        "tazr,tcyj->cyazrj",
        tokens.reshape(tok_rows, dp_size, z_size, rows_z),
        kv_grad.reshape(tok_rows, c_size, y_size, cols_cy),
        preferred_element_type=jnp.float32,
    )
    partner = lax.ppermute(weight_part[1 - core].astype(jnp.bfloat16), "c", [(0, 1), (1, 0)])
    part = weight_part[core] + partner.astype(jnp.float32)
    part = lax.psum_scatter(part.astype(jnp.bfloat16), "y", scatter_dimension=0, tiled=True)[0]
    part = part.astype(jnp.float32).reshape(dp_size * z_size, rows_z, cols_cy)
    part = lax.psum_scatter(part, ("dp", "z"), scatter_dimension=0, tiled=True)
    part = lax.optimization_barrier(part).astype(jnp.bfloat16)
    part = lax.all_gather(part, ("z", "y"), axis=0, tiled=True)
    part = part.reshape(z_size, y_size, rows_z, cols_cy).transpose(1, 0, 2, 3)
    part = lax.all_gather(part.reshape(y_size, row_share, cols_cy), "c", axis=0)
    weight_grad = jnp.transpose(part, (2, 0, 1, 3)).reshape(row_share, 2 * kv_width)
    attended = mixed_half.reshape(1, tok_rows, HQ * HD)
    grad_query = query_grad.astype(jnp.bfloat16).reshape(1, tok_rows, HQ * HD)
    return (
        attended,
        grad_query,
        grad_input.reshape(1, tok_rows, D),
        weight_grad[:, :kv_width],
        weight_grad[:, kv_width:],
    )


def solution(mesh):
    z_size = mesh.devices.shape[1] // 8
    split = jax.sharding.Mesh(
        mesh.devices.reshape(mesh.devices.shape[0], z_size, 4, 2), ("dp",) + CTX
    )
    tokens_spec = P("dp", CTX, None)
    in_specs = (tokens_spec, tokens_spec, P("dp", None), P("dp", None), P("dp", None), tokens_spec)
    out_specs = (tokens_spec, tokens_spec, tokens_spec, P("dp", None), P("dp", None))
    return jax.shard_map(shards, mesh=split, in_specs=in_specs, out_specs=out_specs, check_vma=False)
```

```python
import jax
import jax.numpy as jnp
from jax import lax
from jax.sharding import PartitionSpec as P

D = 2304
HQ = 4
HK = 2
HD = 256
WINDOW = 2048


FLOOR = -1e30
CTX = ("z", "y", "c")


def ctx_size():
    return lax.axis_size("z") * lax.axis_size("y") * lax.axis_size("c")


def from_behind(value, axis, by):
    peers = ctx_size()
    pairs = [(i, i + by) for i in range(peers) if 0 <= i + by < peers]
    return lax.ppermute(value, axis, pairs)


def segment_of(lengths, positions):
    doc_ends = jnp.cumsum(lengths, dtype=jnp.int32)
    return jnp.sum(
        (doc_ends[None, :] <= positions[:, None]).astype(jnp.int32), axis=1, dtype=jnp.int32
    )


def band_mask(query_pos, query_seg, key_pos, key_seg):
    distance_gap = query_pos[:, None] - key_pos[None, :]
    inside = (distance_gap >= 0) & (distance_gap < WINDOW) & (key_pos[None, :] >= 0)
    return inside & (query_seg[:, None] == key_seg[None, :])


def masked_scores(query_heads, key_rows, allowed):
    key_heads = key_rows.reshape(key_rows.shape[0], HK, HD)
    scores = jnp.einsum(
        "qkgd,tkd->kgqt", query_heads, key_heads, preferred_element_type=jnp.float32
    ) * HD ** (-0.5)
    return jnp.where(allowed[None, None], scores, -jnp.inf)


def score_stats(scores):
    highest = jnp.maximum(jnp.max(scores, axis=-1), FLOOR)
    summed = jnp.sum(jnp.exp(scores - highest[..., None]), axis=-1)
    return (highest, summed)


def softmax_of(scores, log_total):
    softmax = jnp.exp(scores - log_total[..., None])
    return (softmax, softmax.astype(jnp.bfloat16))


def values_of(soft_half, value_rows):
    value_heads = value_rows.reshape(value_rows.shape[0], HK, HD)
    return jnp.einsum("kgqt,tkd->qkgd", soft_half, value_heads, preferred_element_type=jnp.float32)


def row_delta(upstream_heads, mixed_half):
    products = upstream_heads.astype(jnp.float32) * mixed_half.astype(jnp.float32)
    return jnp.transpose(jnp.sum(products, axis=-1), (1, 2, 0))


def band_grads(softmax, soft_half, query_heads, upstream_heads, delta_sum, key_rows, value_rows, block_rows):
    span_rows = key_rows.shape[0]
    key_heads = key_rows.reshape(span_rows, HK, HD)
    value_heads = value_rows.reshape(span_rows, HK, HD)
    prob_grad = jnp.einsum(
        "qkgd,tkd->kgqt", upstream_heads, value_heads, preferred_element_type=jnp.float32
    )
    score_grad = (softmax * (prob_grad - delta_sum[..., None]) * HD ** (-0.5)).astype(jnp.bfloat16)
    kv_blocks = []
    for block in range(span_rows // block_rows):
        cols = slice(block * block_rows, (block + 1) * block_rows)
        key_grad = jnp.einsum(
            "kgqt,qkgd->tkd", score_grad[..., cols], query_heads, preferred_element_type=jnp.float32
        )
        value_grad = jnp.einsum(
            "kgqt,qkgd->tkd", soft_half[..., cols], upstream_heads, preferred_element_type=jnp.float32
        )
        kv_blocks.append(
            jnp.concatenate(
                [key_grad.reshape(block_rows, HK * HD), value_grad.reshape(block_rows, HK * HD)], axis=1
            )
        )
    query_grad = jnp.einsum(
        "kgqt,tkd->qkgd", score_grad, key_heads, preferred_element_type=jnp.float32
    )
    return (query_grad, kv_blocks)


def shards(inputs, query, w_key, w_value, doc_lengths, grad_out):
    tokens = inputs[0]
    queries = query[0]
    upstream = grad_out[0]
    lengths = doc_lengths[0]
    tok_rows = tokens.shape[0]
    distant = WINDOW // tok_rows
    per_group = HQ // HK
    kv_width = HK * HD
    core = lax.axis_index("c")
    dp_size = lax.axis_size("dp")
    dp_index = lax.axis_index("dp")
    mine = jnp.stack([w_key, w_value])[core]
    arrived = [mine] + [
        lax.ppermute(mine, "dp", [(i, (i + by) % dp_size) for i in range(dp_size)])
        for by in range(1, dp_size)
    ]
    order = (dp_index - jnp.arange(dp_size, dtype=jnp.int32)) % dp_size
    mine_full = jnp.take(jnp.stack(arrived), order, axis=0).reshape(D, kv_width)
    other_full = lax.ppermute(mine_full, "c", [(0, 1), (1, 0)])
    first = core == 0
    key_full = jnp.where(first, mine_full, other_full)
    value_full = jnp.where(first, other_full, mine_full)
    key_own = jnp.dot(tokens, key_full, preferred_element_type=jnp.float32).astype(jnp.bfloat16)
    value_own = jnp.dot(tokens, value_full, preferred_element_type=jnp.float32).astype(jnp.bfloat16)
    kv_own = jnp.concatenate([key_own, value_own], axis=1)
    earlier = jnp.concatenate(
        [from_behind(kv_own, CTX, distance) for distance in range(distant, 0, -1)], axis=0
    )
    window = jnp.concatenate([earlier, kv_own], axis=0)
    device_index = lax.axis_index(CTX)
    first_row = device_index * tok_rows
    query_pos = first_row + jnp.arange(tok_rows, dtype=jnp.int32)
    key_pos = first_row - distant * tok_rows + jnp.arange((distant + 1) * tok_rows, dtype=jnp.int32)
    allowed = band_mask(
        query_pos, segment_of(lengths, query_pos), key_pos, segment_of(lengths, key_pos)
    )
    query_heads = queries.reshape(tok_rows, HK, per_group, HD)
    upstream_heads = upstream.reshape(tok_rows, HK, per_group, HD)
    scores = masked_scores(query_heads, window[:, :kv_width], allowed)
    highest, summed = score_stats(scores)
    log_total = highest + jnp.log(summed)
    softmax, soft_half = softmax_of(scores, log_total)
    mixed_half = values_of(soft_half, window[:, kv_width:]).astype(jnp.bfloat16)
    delta_sum = row_delta(upstream_heads, mixed_half)
    query_grad, kv_blocks = band_grads(
        softmax,
        soft_half,
        query_heads,
        upstream_heads,
        delta_sum,
        window[:, :kv_width],
        window[:, kv_width:],
        tok_rows,
    )
    own_grad = kv_blocks[distant]
    for distance in range(distant, 0, -1):
        own_grad = own_grad + from_behind(
            kv_blocks[distant - distance].astype(jnp.bfloat16), CTX, -distance
        ).astype(jnp.float32)
    kv_grad = own_grad.astype(jnp.bfloat16)
    grad_input = (
        jnp.dot(kv_grad[:, :kv_width], key_full.T, preferred_element_type=jnp.float32)
        + jnp.dot(kv_grad[:, kv_width:], value_full.T, preferred_element_type=jnp.float32)
    ).astype(jnp.bfloat16)
    z_size, y_size, c_size = lax.axis_size("z"), lax.axis_size("y"), lax.axis_size("c")
    row_share = D // dp_size
    rows_z = row_share // z_size
    cols_cy = 2 * kv_width // (c_size * y_size)
    weight_part = jnp.einsum(
        "tazr,tcyj->cyazrj",
        tokens.reshape(tok_rows, dp_size, z_size, rows_z),
        kv_grad.reshape(tok_rows, c_size, y_size, cols_cy),
        preferred_element_type=jnp.float32,
    )
    partner = lax.ppermute(weight_part[1 - core].astype(jnp.bfloat16), "c", [(0, 1), (1, 0)])
    part = weight_part[core] + partner.astype(jnp.float32)
    part = lax.psum_scatter(part.astype(jnp.bfloat16), "y", scatter_dimension=0, tiled=True)[0]
    part = part.astype(jnp.float32)
    step = 1
    while step < dp_size:
        bit = (dp_index // step) % 2
        split = part.reshape(part.shape[0] // 2, 2, *part.shape[1:])
        sent = lax.ppermute(split[:, 1 - bit], "dp", [(i, i ^ step) for i in range(dp_size)])
        part = split[:, bit] + sent
        step *= 2
    part = part[0]
    step = 1
    while step < z_size:
        part = part + lax.ppermute(part, "z", [(i, i ^ step) for i in range(z_size)])
        step *= 2
    part = part.astype(jnp.bfloat16).reshape(row_share, cols_cy)
    part = lax.all_gather(part, "y", axis=0)
    part = lax.all_gather(part, "c", axis=0)
    weight_grad = jnp.transpose(part, (2, 0, 1, 3)).reshape(row_share, 2 * kv_width)
    attended = mixed_half.reshape(1, tok_rows, HQ * HD)
    grad_query = query_grad.astype(jnp.bfloat16).reshape(1, tok_rows, HQ * HD)
    return (
        attended,
        grad_query,
        grad_input.reshape(1, tok_rows, D),
        weight_grad[:, :kv_width],
        weight_grad[:, kv_width:],
    )


def solution(mesh):
    z_size = mesh.devices.shape[1] // 8
    split = jax.sharding.Mesh(
        mesh.devices.reshape(mesh.devices.shape[0], z_size, 4, 2), ("dp",) + CTX
    )
    tokens_spec = P("dp", CTX, None)
    in_specs = (tokens_spec, tokens_spec, P("dp", None), P("dp", None), P("dp", None), tokens_spec)
    out_specs = (tokens_spec, tokens_spec, tokens_spec, P("dp", None), P("dp", None))
    return jax.shard_map(shards, mesh=split, in_specs=in_specs, out_specs=out_specs, check_vma=False)
```

```python
import jax
import jax.numpy as jnp
from jax import lax
from jax.sharding import PartitionSpec as P

D = 2304
HQ = 4
HK = 2
HD = 256
WINDOW = 2048


FLOOR = -1e30
CTX = ("z", "y", "c")


def ctx_size():
    return lax.axis_size("z") * lax.axis_size("y") * lax.axis_size("c")


def from_behind(value, axis, by):
    peers = ctx_size()
    pairs = [(i, i + by) for i in range(peers) if 0 <= i + by < peers]
    return lax.ppermute(value, axis, pairs)


def segment_of(lengths, positions):
    doc_ends = jnp.cumsum(lengths, dtype=jnp.int32)
    return jnp.sum(
        (doc_ends[None, :] <= positions[:, None]).astype(jnp.int32), axis=1, dtype=jnp.int32
    )


def band_mask(query_pos, query_seg, key_pos, key_seg):
    distance_gap = query_pos[:, None] - key_pos[None, :]
    inside = (distance_gap >= 0) & (distance_gap < WINDOW) & (key_pos[None, :] >= 0)
    return inside & (query_seg[:, None] == key_seg[None, :])


def masked_scores(query_heads, key_rows, allowed):
    key_heads = key_rows.reshape(key_rows.shape[0], HK, HD)
    scores = jnp.einsum(
        "qkgd,tkd->kgqt", query_heads, key_heads, preferred_element_type=jnp.float32
    ) * HD ** (-0.5)
    return jnp.where(allowed[None, None], scores, -jnp.inf)


def score_stats(scores):
    highest = jnp.maximum(jnp.max(scores, axis=-1), FLOOR)
    summed = jnp.sum(jnp.exp(scores - highest[..., None]), axis=-1)
    return (highest, summed)


def softmax_of(scores, log_total):
    softmax = jnp.exp(scores - log_total[..., None])
    return (softmax, softmax.astype(jnp.bfloat16))


def values_of(soft_half, value_rows):
    value_heads = value_rows.reshape(value_rows.shape[0], HK, HD)
    return jnp.einsum("kgqt,tkd->qkgd", soft_half, value_heads, preferred_element_type=jnp.float32)


def row_delta(upstream_heads, mixed_half):
    products = upstream_heads.astype(jnp.float32) * mixed_half.astype(jnp.float32)
    return jnp.transpose(jnp.sum(products, axis=-1), (1, 2, 0))


def band_grads(softmax, soft_half, query_heads, upstream_heads, delta_sum, key_rows, value_rows, block_rows):
    span_rows = key_rows.shape[0]
    key_heads = key_rows.reshape(span_rows, HK, HD)
    value_heads = value_rows.reshape(span_rows, HK, HD)
    prob_grad = jnp.einsum(
        "qkgd,tkd->kgqt", upstream_heads, value_heads, preferred_element_type=jnp.float32
    )
    score_grad = (softmax * (prob_grad - delta_sum[..., None]) * HD ** (-0.5)).astype(jnp.bfloat16)
    kv_blocks = []
    for block in range(span_rows // block_rows):
        cols = slice(block * block_rows, (block + 1) * block_rows)
        key_grad = jnp.einsum(
            "kgqt,qkgd->tkd", score_grad[..., cols], query_heads, preferred_element_type=jnp.float32
        )
        value_grad = jnp.einsum(
            "kgqt,qkgd->tkd", soft_half[..., cols], upstream_heads, preferred_element_type=jnp.float32
        )
        kv_blocks.append(
            jnp.concatenate(
                [key_grad.reshape(block_rows, HK * HD), value_grad.reshape(block_rows, HK * HD)], axis=1
            )
        )
    query_grad = jnp.einsum(
        "kgqt,tkd->qkgd", score_grad, key_heads, preferred_element_type=jnp.float32
    )
    return (query_grad, kv_blocks)


def shards(inputs, query, w_key, w_value, doc_lengths, grad_out):
    tokens = inputs[0]
    queries = query[0]
    upstream = grad_out[0]
    lengths = doc_lengths[0]
    tok_rows = tokens.shape[0]
    distant = WINDOW // tok_rows
    per_group = HQ // HK
    kv_width = HK * HD
    core = lax.axis_index("c")
    dp_size = lax.axis_size("dp")
    dp_index = lax.axis_index("dp")
    mine = jnp.stack([w_key, w_value])[core]
    arrived = [mine] + [
        lax.ppermute(mine, "dp", [(i, (i + by) % dp_size) for i in range(dp_size)])
        for by in range(1, dp_size)
    ]
    order = (dp_index - jnp.arange(dp_size, dtype=jnp.int32)) % dp_size
    mine_full = jnp.take(jnp.stack(arrived), order, axis=0).reshape(D, kv_width)
    other_full = lax.ppermute(mine_full, "c", [(0, 1), (1, 0)])
    first = core == 0
    key_full = jnp.where(first, mine_full, other_full)
    value_full = jnp.where(first, other_full, mine_full)
    key_own = jnp.dot(tokens, key_full, preferred_element_type=jnp.float32).astype(jnp.bfloat16)
    value_own = jnp.dot(tokens, value_full, preferred_element_type=jnp.float32).astype(jnp.bfloat16)
    kv_own = jnp.concatenate([key_own, value_own], axis=1)
    chips_back = distant // 2
    swap = [(0, 1), (1, 0)]
    fetched = [kv_own] + [from_behind(kv_own, CTX, 2 * back) for back in range(1, chips_back + 1)]
    partner_kv = lax.ppermute(jnp.stack(fetched), "c", swap)
    blocks = []
    for back in range(chips_back, 0, -1):
        blocks += [fetched[back], partner_kv[back - core]]
    window = jnp.concatenate(blocks + [kv_own], axis=0)
    device_index = lax.axis_index(CTX)
    first_row = device_index * tok_rows
    query_pos = first_row + jnp.arange(tok_rows, dtype=jnp.int32)
    key_pos = first_row - distant * tok_rows + jnp.arange((distant + 1) * tok_rows, dtype=jnp.int32)
    allowed = band_mask(
        query_pos, segment_of(lengths, query_pos), key_pos, segment_of(lengths, key_pos)
    )
    query_heads = queries.reshape(tok_rows, HK, per_group, HD)
    upstream_heads = upstream.reshape(tok_rows, HK, per_group, HD)
    scores = masked_scores(query_heads, window[:, :kv_width], allowed)
    highest, summed = score_stats(scores)
    log_total = highest + jnp.log(summed)
    softmax, soft_half = softmax_of(scores, log_total)
    mixed_half = values_of(soft_half, window[:, kv_width:]).astype(jnp.bfloat16)
    delta_sum = row_delta(upstream_heads, mixed_half)
    query_grad, kv_blocks = band_grads(
        softmax,
        soft_half,
        query_heads,
        upstream_heads,
        delta_sum,
        window[:, :kv_width],
        window[:, kv_width:],
        tok_rows,
    )
    crossed = jnp.stack(
        [kv_blocks[distant + 1 - 2 * back].astype(jnp.bfloat16) for back in range(1, chips_back + 1)]
    )
    from_partner = lax.ppermute(crossed, "c", swap).astype(jnp.float32)
    padded = jnp.concatenate([jnp.zeros_like(from_partner[:1]), from_partner, jnp.zeros_like(from_partner[:1])])
    own_grad = kv_blocks[distant] + padded[1 - core]
    for back in range(chips_back, 0, -1):
        mine_total = kv_blocks[distant - 2 * back] + padded[back + 1 - core]
        own_grad = own_grad + from_behind(
            mine_total.astype(jnp.bfloat16), CTX, -2 * back
        ).astype(jnp.float32)
    kv_grad = own_grad.astype(jnp.bfloat16)
    grad_input = (
        jnp.dot(kv_grad[:, :kv_width], key_full.T, preferred_element_type=jnp.float32)
        + jnp.dot(kv_grad[:, kv_width:], value_full.T, preferred_element_type=jnp.float32)
    ).astype(jnp.bfloat16)
    z_size, y_size, c_size = lax.axis_size("z"), lax.axis_size("y"), lax.axis_size("c")
    row_share = D // dp_size
    rows_z = row_share // z_size
    cols_cy = 2 * kv_width // (c_size * y_size)
    weight_part = jnp.einsum(
        "tazr,tcyj->cyazrj",
        tokens.reshape(tok_rows, dp_size, z_size, rows_z),
        kv_grad.reshape(tok_rows, c_size, y_size, cols_cy),
        preferred_element_type=jnp.float32,
    )
    partner = lax.ppermute(weight_part[1 - core].astype(jnp.bfloat16), "c", [(0, 1), (1, 0)])
    part = weight_part[core] + partner.astype(jnp.float32)
    part = lax.psum_scatter(part.astype(jnp.bfloat16), "y", scatter_dimension=0, tiled=True)[0]
    part = part.astype(jnp.float32)
    step = 1
    while step < dp_size:
        bit = (dp_index // step) % 2
        split = part.reshape(part.shape[0] // 2, 2, *part.shape[1:])
        sent = lax.ppermute(split[:, 1 - bit], "dp", [(i, i ^ step) for i in range(dp_size)])
        part = split[:, bit] + sent
        step *= 2
    part = part[0]
    step = 1
    while step < z_size:
        part = part + lax.ppermute(part, "z", [(i, i ^ step) for i in range(z_size)])
        step *= 2
    part = part.astype(jnp.bfloat16).reshape(row_share, cols_cy)
    part = lax.all_gather(part, "y", axis=0)
    part = lax.all_gather(part, "c", axis=0)
    weight_grad = jnp.transpose(part, (2, 0, 1, 3)).reshape(row_share, 2 * kv_width)
    attended = mixed_half.reshape(1, tok_rows, HQ * HD)
    grad_query = query_grad.astype(jnp.bfloat16).reshape(1, tok_rows, HQ * HD)
    return (
        attended,
        grad_query,
        grad_input.reshape(1, tok_rows, D),
        weight_grad[:, :kv_width],
        weight_grad[:, kv_width:],
    )


def solution(mesh):
    z_size = mesh.devices.shape[1] // 8
    split = jax.sharding.Mesh(
        mesh.devices.reshape(mesh.devices.shape[0], z_size, 4, 2), ("dp",) + CTX
    )
    tokens_spec = P("dp", CTX, None)
    in_specs = (tokens_spec, tokens_spec, P("dp", None), P("dp", None), P("dp", None), tokens_spec)
    out_specs = (tokens_spec, tokens_spec, tokens_spec, P("dp", None), P("dp", None))
    return jax.shard_map(shards, mesh=split, in_specs=in_specs, out_specs=out_specs, check_vma=False)
```

```python
import jax
import jax.numpy as jnp
from jax import lax
from jax.sharding import PartitionSpec as P

D = 2304
HQ = 4
HK = 2
HD = 256
WINDOW = 2048


FLOOR = -1e30
CTX = ("z", "y", "c")


def ctx_size():
    return lax.axis_size("z") * lax.axis_size("y") * lax.axis_size("c")


def from_behind(value, axis, by):
    peers = ctx_size()
    pairs = [(i, i + by) for i in range(peers) if 0 <= i + by < peers]
    return lax.ppermute(value, axis, pairs)


def segment_of(lengths, positions):
    doc_ends = jnp.cumsum(lengths, dtype=jnp.int32)
    return jnp.sum(
        (doc_ends[None, :] <= positions[:, None]).astype(jnp.int32), axis=1, dtype=jnp.int32
    )


def band_mask(query_pos, query_seg, key_pos, key_seg):
    distance_gap = query_pos[:, None] - key_pos[None, :]
    inside = (distance_gap >= 0) & (distance_gap < WINDOW) & (key_pos[None, :] >= 0)
    return inside & (query_seg[:, None] == key_seg[None, :])


def masked_scores(query_heads, key_rows, allowed):
    key_heads = key_rows.reshape(key_rows.shape[0], HK, HD)
    scores = jnp.einsum(
        "qkgd,tkd->kgqt", query_heads, key_heads, preferred_element_type=jnp.float32
    ) * HD ** (-0.5)
    return jnp.where(allowed[None, None], scores, -jnp.inf)


def score_stats(scores):
    highest = jnp.maximum(jnp.max(scores, axis=-1), FLOOR)
    summed = jnp.sum(jnp.exp(scores - highest[..., None]), axis=-1)
    return (highest, summed)


def softmax_of(scores, log_total):
    softmax = jnp.exp(scores - log_total[..., None])
    return (softmax, softmax.astype(jnp.bfloat16))


def values_of(soft_half, value_rows):
    value_heads = value_rows.reshape(value_rows.shape[0], HK, HD)
    return jnp.einsum("kgqt,tkd->qkgd", soft_half, value_heads, preferred_element_type=jnp.float32)


def row_delta(upstream_heads, mixed_half):
    products = upstream_heads.astype(jnp.float32) * mixed_half.astype(jnp.float32)
    return jnp.transpose(jnp.sum(products, axis=-1), (1, 2, 0))


def band_grads(softmax, soft_half, query_heads, upstream_heads, delta_sum, key_rows, value_rows, block_rows):
    span_rows = key_rows.shape[0]
    key_heads = key_rows.reshape(span_rows, HK, HD)
    value_heads = value_rows.reshape(span_rows, HK, HD)
    prob_grad = jnp.einsum(
        "qkgd,tkd->kgqt", upstream_heads, value_heads, preferred_element_type=jnp.float32
    )
    score_grad = (softmax * (prob_grad - delta_sum[..., None]) * HD ** (-0.5)).astype(jnp.bfloat16)
    kv_blocks = []
    for block in range(span_rows // block_rows):
        cols = slice(block * block_rows, (block + 1) * block_rows)
        key_grad = jnp.einsum(
            "kgqt,qkgd->tkd", score_grad[..., cols], query_heads, preferred_element_type=jnp.float32
        )
        value_grad = jnp.einsum(
            "kgqt,qkgd->tkd", soft_half[..., cols], upstream_heads, preferred_element_type=jnp.float32
        )
        kv_blocks.append(
            jnp.concatenate(
                [key_grad.reshape(block_rows, HK * HD), value_grad.reshape(block_rows, HK * HD)], axis=1
            )
        )
    query_grad = jnp.einsum(
        "kgqt,tkd->qkgd", score_grad, key_heads, preferred_element_type=jnp.float32
    )
    return (query_grad, kv_blocks)


def shards(inputs, query, w_key, w_value, doc_lengths, grad_out):
    tokens = inputs[0]
    queries = query[0]
    upstream = grad_out[0]
    lengths = doc_lengths[0]
    tok_rows = tokens.shape[0]
    distant = WINDOW // tok_rows
    per_group = HQ // HK
    kv_width = HK * HD
    core = lax.axis_index("c")
    dp_size = lax.axis_size("dp")
    dp_index = lax.axis_index("dp")
    mine = jnp.stack([w_key, w_value])[core]
    arrived = [mine] + [
        lax.ppermute(mine, "dp", [(i, (i + by) % dp_size) for i in range(dp_size)])
        for by in range(1, dp_size)
    ]
    order = (dp_index - jnp.arange(dp_size, dtype=jnp.int32)) % dp_size
    mine_full = jnp.take(jnp.stack(arrived), order, axis=0).reshape(D, kv_width)
    other_full = lax.ppermute(mine_full, "c", [(0, 1), (1, 0)])
    first = core == 0
    key_full = jnp.where(first, mine_full, other_full)
    value_full = jnp.where(first, other_full, mine_full)
    key_own = jnp.dot(tokens, key_full, preferred_element_type=jnp.float32).astype(jnp.bfloat16)
    value_own = jnp.dot(tokens, value_full, preferred_element_type=jnp.float32).astype(jnp.bfloat16)
    kv_own = jnp.concatenate([key_own, value_own], axis=1)
    chips_back = distant // 2
    swap = [(0, 1), (1, 0)]
    fetched = [kv_own] + [from_behind(kv_own, CTX, 2 * back) for back in range(1, chips_back + 1)]
    partner_kv = lax.ppermute(jnp.stack(fetched), "c", swap)
    blocks = []
    for back in range(chips_back, 0, -1):
        blocks += [fetched[back], partner_kv[back - core]]
    window = jnp.concatenate(blocks + [kv_own], axis=0)
    device_index = lax.axis_index(CTX)
    first_row = device_index * tok_rows
    query_pos = first_row + jnp.arange(tok_rows, dtype=jnp.int32)
    key_pos = first_row - distant * tok_rows + jnp.arange((distant + 1) * tok_rows, dtype=jnp.int32)
    allowed = band_mask(
        query_pos, segment_of(lengths, query_pos), key_pos, segment_of(lengths, key_pos)
    )
    query_heads = queries.reshape(tok_rows, HK, per_group, HD)
    upstream_heads = upstream.reshape(tok_rows, HK, per_group, HD)
    scores = masked_scores(query_heads, window[:, :kv_width], allowed)
    highest, summed = score_stats(scores)
    log_total = highest + jnp.log(summed)
    softmax, soft_half = softmax_of(scores, log_total)
    mixed_half = values_of(soft_half, window[:, kv_width:]).astype(jnp.bfloat16)
    delta_sum = row_delta(upstream_heads, mixed_half)
    query_grad, kv_blocks = band_grads(
        softmax,
        soft_half,
        query_heads,
        upstream_heads,
        delta_sum,
        window[:, :kv_width],
        window[:, kv_width:],
        tok_rows,
    )
    crossed = jnp.stack(
        [kv_blocks[distant + 1 - 2 * back].astype(jnp.bfloat16) for back in range(1, chips_back + 1)]
    )
    from_partner = lax.ppermute(crossed, "c", swap).astype(jnp.float32)
    padded = jnp.concatenate([jnp.zeros_like(from_partner[:1]), from_partner, jnp.zeros_like(from_partner[:1])])
    own_grad = kv_blocks[distant] + padded[1 - core]
    for back in range(chips_back, 0, -1):
        mine_total = kv_blocks[distant - 2 * back] + padded[back + 1 - core]
        own_grad = own_grad + from_behind(
            mine_total.astype(jnp.bfloat16), CTX, -2 * back
        ).astype(jnp.float32)
    kv_grad = own_grad.astype(jnp.bfloat16)
    grad_input = (
        jnp.dot(kv_grad[:, :kv_width], key_full.T, preferred_element_type=jnp.float32)
        + jnp.dot(kv_grad[:, kv_width:], value_full.T, preferred_element_type=jnp.float32)
    ).astype(jnp.bfloat16)
    z_size, y_size, c_size = lax.axis_size("z"), lax.axis_size("y"), lax.axis_size("c")
    row_share = D // dp_size
    rows_z = row_share // z_size
    cols_cy = 2 * kv_width // (c_size * y_size)
    weight_part = jnp.einsum(
        "tazr,tcyj->cyazrj",
        tokens.reshape(tok_rows, dp_size, z_size, rows_z),
        kv_grad.reshape(tok_rows, c_size, y_size, cols_cy),
        preferred_element_type=jnp.float32,
    )
    partner = lax.ppermute(weight_part[1 - core].astype(jnp.bfloat16), "c", [(0, 1), (1, 0)])
    part = weight_part[core] + partner.astype(jnp.float32)
    part = lax.psum_scatter(part.astype(jnp.bfloat16), "y", scatter_dimension=0, tiled=True)[0]
    part = part.astype(jnp.float32)
    step = 1
    while step < dp_size:
        bit = (dp_index // step) % 2
        split = part.reshape(part.shape[0] // 2, 2, *part.shape[1:])
        sent = lax.ppermute(
            split[:, 1 - bit].astype(jnp.bfloat16), "dp", [(i, i ^ step) for i in range(dp_size)]
        )
        part = split[:, bit] + sent.astype(jnp.float32)
        step *= 2
    part = part[0]
    step = 1
    while step < z_size:
        half = part.astype(jnp.bfloat16)
        part = half.astype(jnp.float32) + lax.ppermute(
            half, "z", [(i, i ^ step) for i in range(z_size)]
        ).astype(jnp.float32)
        step *= 2
    part = part.astype(jnp.bfloat16).reshape(row_share, cols_cy)
    part = lax.all_gather(part, "y", axis=0)
    part = lax.all_gather(part, "c", axis=0)
    weight_grad = jnp.transpose(part, (2, 0, 1, 3)).reshape(row_share, 2 * kv_width)
    attended = mixed_half.reshape(1, tok_rows, HQ * HD)
    grad_query = query_grad.astype(jnp.bfloat16).reshape(1, tok_rows, HQ * HD)
    return (
        attended,
        grad_query,
        grad_input.reshape(1, tok_rows, D),
        weight_grad[:, :kv_width],
        weight_grad[:, kv_width:],
    )


def solution(mesh):
    z_size = mesh.devices.shape[1] // 8
    split = jax.sharding.Mesh(
        mesh.devices.reshape(mesh.devices.shape[0], z_size, 4, 2), ("dp",) + CTX
    )
    tokens_spec = P("dp", CTX, None)
    in_specs = (tokens_spec, tokens_spec, P("dp", None), P("dp", None), P("dp", None), tokens_spec)
    out_specs = (tokens_spec, tokens_spec, tokens_spec, P("dp", None), P("dp", None))
    return jax.shard_map(shards, mesh=split, in_specs=in_specs, out_specs=out_specs, check_vma=False)
```

```python
import jax
import jax.numpy as jnp
from jax import lax
from jax.sharding import PartitionSpec as P

D = 2304
HQ = 4
HK = 2
HD = 256
WINDOW = 2048


FLOOR = -1e30
CTX = ("z", "y", "c")


def ctx_size():
    return lax.axis_size("z") * lax.axis_size("y") * lax.axis_size("c")


def from_behind(value, axis, by):
    peers = ctx_size()
    pairs = [(i, i + by) for i in range(peers) if 0 <= i + by < peers]
    return lax.ppermute(value, axis, pairs)


def halve(part, axis, size):
    index = lax.axis_index(axis)
    step = 1
    while step < size:
        bit = (index // step) % 2
        split = part.reshape(part.shape[0] // 2, 2, *part.shape[1:])
        sent = lax.ppermute(
            split[:, 1 - bit].astype(jnp.bfloat16), axis, [(i, i ^ step) for i in range(size)]
        )
        part = split[:, bit] + sent.astype(jnp.float32)
        step *= 2
    return part


def double(held, axis, size):
    index = lax.axis_index(axis)
    step = 1
    while step < size:
        low = (index // step) % 2 == 0
        other = lax.ppermute(held, axis, [(i, i ^ step) for i in range(size)])
        held = jnp.where(
            low, jnp.concatenate([held, other]), jnp.concatenate([other, held])
        )
        step *= 2
    return held


def segment_of(lengths, positions):
    doc_ends = jnp.cumsum(lengths, dtype=jnp.int32)
    return jnp.sum(
        (doc_ends[None, :] <= positions[:, None]).astype(jnp.int32), axis=1, dtype=jnp.int32
    )


def band_mask(query_pos, query_seg, key_pos, key_seg):
    distance_gap = query_pos[:, None] - key_pos[None, :]
    inside = (distance_gap >= 0) & (distance_gap < WINDOW) & (key_pos[None, :] >= 0)
    return inside & (query_seg[:, None] == key_seg[None, :])


def masked_scores(query_heads, key_rows, allowed):
    key_heads = key_rows.reshape(key_rows.shape[0], HK, HD)
    scores = jnp.einsum(
        "qkgd,tkd->kgqt", query_heads, key_heads, preferred_element_type=jnp.float32
    ) * HD ** (-0.5)
    return jnp.where(allowed[None, None], scores, -jnp.inf)


def score_stats(scores):
    highest = jnp.maximum(jnp.max(scores, axis=-1), FLOOR)
    summed = jnp.sum(jnp.exp(scores - highest[..., None]), axis=-1)
    return (highest, summed)


def softmax_of(scores, log_total):
    softmax = jnp.exp(scores - log_total[..., None])
    return (softmax, softmax.astype(jnp.bfloat16))


def values_of(soft_half, value_rows):
    value_heads = value_rows.reshape(value_rows.shape[0], HK, HD)
    return jnp.einsum("kgqt,tkd->qkgd", soft_half, value_heads, preferred_element_type=jnp.float32)


def row_delta(upstream_heads, mixed_half):
    products = upstream_heads.astype(jnp.float32) * mixed_half.astype(jnp.float32)
    return jnp.transpose(jnp.sum(products, axis=-1), (1, 2, 0))


def band_grads(softmax, soft_half, query_heads, upstream_heads, delta_sum, key_rows, value_rows, block_rows):
    span_rows = key_rows.shape[0]
    key_heads = key_rows.reshape(span_rows, HK, HD)
    value_heads = value_rows.reshape(span_rows, HK, HD)
    prob_grad = jnp.einsum(
        "qkgd,tkd->kgqt", upstream_heads, value_heads, preferred_element_type=jnp.float32
    )
    score_grad = (softmax * (prob_grad - delta_sum[..., None]) * HD ** (-0.5)).astype(jnp.bfloat16)
    kv_blocks = []
    for block in range(span_rows // block_rows):
        cols = slice(block * block_rows, (block + 1) * block_rows)
        key_grad = jnp.einsum(
            "kgqt,qkgd->tkd", score_grad[..., cols], query_heads, preferred_element_type=jnp.float32
        )
        value_grad = jnp.einsum(
            "kgqt,qkgd->tkd", soft_half[..., cols], upstream_heads, preferred_element_type=jnp.float32
        )
        kv_blocks.append(
            jnp.concatenate(
                [key_grad.reshape(block_rows, HK * HD), value_grad.reshape(block_rows, HK * HD)], axis=1
            )
        )
    query_grad = jnp.einsum(
        "kgqt,tkd->qkgd", score_grad, key_heads, preferred_element_type=jnp.float32
    )
    return (query_grad, kv_blocks)


def shards(inputs, query, w_key, w_value, doc_lengths, grad_out):
    tokens = inputs[0]
    queries = query[0]
    upstream = grad_out[0]
    lengths = doc_lengths[0]
    tok_rows = tokens.shape[0]
    distant = WINDOW // tok_rows
    per_group = HQ // HK
    kv_width = HK * HD
    core = lax.axis_index("c")
    dp_size = lax.axis_size("dp")
    dp_index = lax.axis_index("dp")
    mine = jnp.stack([w_key, w_value])[core]
    arrived = [mine] + [
        lax.ppermute(mine, "dp", [(i, (i + by) % dp_size) for i in range(dp_size)])
        for by in range(1, dp_size)
    ]
    order = (dp_index - jnp.arange(dp_size, dtype=jnp.int32)) % dp_size
    mine_full = jnp.take(jnp.stack(arrived), order, axis=0).reshape(D, kv_width)
    other_full = lax.ppermute(mine_full, "c", [(0, 1), (1, 0)])
    first = core == 0
    key_full = jnp.where(first, mine_full, other_full)
    value_full = jnp.where(first, other_full, mine_full)
    key_own = jnp.dot(tokens, key_full, preferred_element_type=jnp.float32).astype(jnp.bfloat16)
    value_own = jnp.dot(tokens, value_full, preferred_element_type=jnp.float32).astype(jnp.bfloat16)
    kv_own = jnp.concatenate([key_own, value_own], axis=1)
    chips_back = distant // 2
    swap = [(0, 1), (1, 0)]
    fetched = [kv_own] + [from_behind(kv_own, CTX, 2 * back) for back in range(1, chips_back + 1)]
    partner_kv = lax.ppermute(jnp.stack(fetched), "c", swap)
    blocks = []
    for back in range(chips_back, 0, -1):
        blocks += [fetched[back], partner_kv[back - core]]
    window = jnp.concatenate(blocks + [kv_own], axis=0)
    device_index = lax.axis_index(CTX)
    first_row = device_index * tok_rows
    query_pos = first_row + jnp.arange(tok_rows, dtype=jnp.int32)
    key_pos = first_row - distant * tok_rows + jnp.arange((distant + 1) * tok_rows, dtype=jnp.int32)
    allowed = band_mask(
        query_pos, segment_of(lengths, query_pos), key_pos, segment_of(lengths, key_pos)
    )
    query_heads = queries.reshape(tok_rows, HK, per_group, HD)
    upstream_heads = upstream.reshape(tok_rows, HK, per_group, HD)
    scores = masked_scores(query_heads, window[:, :kv_width], allowed)
    highest, summed = score_stats(scores)
    log_total = highest + jnp.log(summed)
    softmax, soft_half = softmax_of(scores, log_total)
    mixed_half = values_of(soft_half, window[:, kv_width:]).astype(jnp.bfloat16)
    delta_sum = row_delta(upstream_heads, mixed_half)
    query_grad, kv_blocks = band_grads(
        softmax,
        soft_half,
        query_heads,
        upstream_heads,
        delta_sum,
        window[:, :kv_width],
        window[:, kv_width:],
        tok_rows,
    )
    crossed = jnp.stack(
        [kv_blocks[distant + 1 - 2 * back].astype(jnp.bfloat16) for back in range(1, chips_back + 1)]
    )
    from_partner = lax.ppermute(crossed, "c", swap).astype(jnp.float32)
    padded = jnp.concatenate([jnp.zeros_like(from_partner[:1]), from_partner, jnp.zeros_like(from_partner[:1])])
    own_grad = kv_blocks[distant] + padded[1 - core]
    for back in range(chips_back, 0, -1):
        mine_total = kv_blocks[distant - 2 * back] + padded[back + 1 - core]
        own_grad = own_grad + from_behind(
            mine_total.astype(jnp.bfloat16), CTX, -2 * back
        ).astype(jnp.float32)
    kv_grad = own_grad.astype(jnp.bfloat16)
    grad_input = (
        jnp.dot(kv_grad[:, :kv_width], key_full.T, preferred_element_type=jnp.float32)
        + jnp.dot(kv_grad[:, kv_width:], value_full.T, preferred_element_type=jnp.float32)
    ).astype(jnp.bfloat16)
    z_size, y_size, c_size = lax.axis_size("z"), lax.axis_size("y"), lax.axis_size("c")
    row_share = D // dp_size
    rows_z = row_share // z_size
    cols_cy = 2 * kv_width // (c_size * y_size)
    weight_part = jnp.einsum(
        "tazr,tcyj->cyazrj",
        tokens.reshape(tok_rows, dp_size, z_size, rows_z),
        kv_grad.reshape(tok_rows, c_size, y_size, cols_cy),
        preferred_element_type=jnp.float32,
    )
    partner = lax.ppermute(weight_part[1 - core].astype(jnp.bfloat16), "c", [(0, 1), (1, 0)])
    part = weight_part[core] + partner.astype(jnp.float32)
    part = halve(part, "y", y_size)[0]
    part = halve(part, "dp", dp_size)[0]
    step = 1
    while step < z_size:
        half = part.astype(jnp.bfloat16)
        part = half.astype(jnp.float32) + lax.ppermute(
            half, "z", [(i, i ^ step) for i in range(z_size)]
        ).astype(jnp.float32)
        step *= 2
    part = part.astype(jnp.bfloat16).reshape(row_share, cols_cy)
    part = double(part[None], "y", y_size)
    part = double(part[None], "c", c_size)
    weight_grad = jnp.transpose(part, (2, 0, 1, 3)).reshape(row_share, 2 * kv_width)
    attended = mixed_half.reshape(1, tok_rows, HQ * HD)
    grad_query = query_grad.astype(jnp.bfloat16).reshape(1, tok_rows, HQ * HD)
    return (
        attended,
        grad_query,
        grad_input.reshape(1, tok_rows, D),
        weight_grad[:, :kv_width],
        weight_grad[:, kv_width:],
    )


def solution(mesh):
    z_size = mesh.devices.shape[1] // 8
    split = jax.sharding.Mesh(
        mesh.devices.reshape(mesh.devices.shape[0], z_size, 4, 2), ("dp",) + CTX
    )
    tokens_spec = P("dp", CTX, None)
    in_specs = (tokens_spec, tokens_spec, P("dp", None), P("dp", None), P("dp", None), tokens_spec)
    out_specs = (tokens_spec, tokens_spec, tokens_spec, P("dp", None), P("dp", None))
    return jax.shard_map(shards, mesh=split, in_specs=in_specs, out_specs=out_specs, check_vma=False)
```

```python
import jax
import jax.numpy as jnp
from jax import lax
from jax.sharding import PartitionSpec as P

D = 2304
HQ = 4
HK = 2
HD = 256
WINDOW = 2048


FLOOR = -1e30
CTX = ("z", "y", "c")


def ctx_size():
    return lax.axis_size("z") * lax.axis_size("y") * lax.axis_size("c")


def from_behind(value, axis, by):
    peers = ctx_size()
    pairs = [(i, i + by) for i in range(peers) if 0 <= i + by < peers]
    return lax.ppermute(value, axis, pairs)


def segment_of(lengths, positions):
    doc_ends = jnp.cumsum(lengths, dtype=jnp.int32)
    return jnp.sum(
        (doc_ends[None, :] <= positions[:, None]).astype(jnp.int32), axis=1, dtype=jnp.int32
    )


def band_mask(query_pos, query_seg, key_pos, key_seg):
    distance_gap = query_pos[:, None] - key_pos[None, :]
    inside = (distance_gap >= 0) & (distance_gap < WINDOW) & (key_pos[None, :] >= 0)
    return inside & (query_seg[:, None] == key_seg[None, :])


def masked_scores(query_heads, key_rows, allowed):
    key_heads = key_rows.reshape(key_rows.shape[0], HK, HD)
    scores = jnp.einsum(
        "qkgd,tkd->kgqt", query_heads, key_heads, preferred_element_type=jnp.float32
    ) * HD ** (-0.5)
    return jnp.where(allowed[None, None], scores, -jnp.inf)


def score_stats(scores):
    highest = jnp.maximum(jnp.max(scores, axis=-1), FLOOR)
    summed = jnp.sum(jnp.exp(scores - highest[..., None]), axis=-1)
    return (highest, summed)


def softmax_of(scores, log_total):
    softmax = jnp.exp(scores - log_total[..., None])
    return (softmax, softmax.astype(jnp.bfloat16))


def values_of(soft_half, value_rows):
    value_heads = value_rows.reshape(value_rows.shape[0], HK, HD)
    return jnp.einsum("kgqt,tkd->qkgd", soft_half, value_heads, preferred_element_type=jnp.float32)


def row_delta(upstream_heads, mixed_half):
    products = upstream_heads.astype(jnp.float32) * mixed_half.astype(jnp.float32)
    return jnp.transpose(jnp.sum(products, axis=-1), (1, 2, 0))


def band_grads(softmax, soft_half, query_heads, upstream_heads, delta_sum, key_rows, value_rows, block_rows):
    span_rows = key_rows.shape[0]
    key_heads = key_rows.reshape(span_rows, HK, HD)
    value_heads = value_rows.reshape(span_rows, HK, HD)
    prob_grad = jnp.einsum(
        "qkgd,tkd->kgqt", upstream_heads, value_heads, preferred_element_type=jnp.float32
    )
    score_grad = (softmax * (prob_grad - delta_sum[..., None]) * HD ** (-0.5)).astype(jnp.bfloat16)
    kv_blocks = []
    for block in range(span_rows // block_rows):
        cols = slice(block * block_rows, (block + 1) * block_rows)
        key_grad = jnp.einsum(
            "kgqt,qkgd->tkd", score_grad[..., cols], query_heads, preferred_element_type=jnp.float32
        )
        value_grad = jnp.einsum(
            "kgqt,qkgd->tkd", soft_half[..., cols], upstream_heads, preferred_element_type=jnp.float32
        )
        kv_blocks.append(
            jnp.concatenate(
                [key_grad.reshape(block_rows, HK * HD), value_grad.reshape(block_rows, HK * HD)], axis=1
            )
        )
    query_grad = jnp.einsum(
        "kgqt,tkd->qkgd", score_grad, key_heads, preferred_element_type=jnp.float32
    )
    return (query_grad, kv_blocks)


def shards(inputs, query, w_key, w_value, doc_lengths, grad_out):
    tokens = inputs[0]
    queries = query[0]
    upstream = grad_out[0]
    lengths = doc_lengths[0]
    tok_rows = tokens.shape[0]
    distant = WINDOW // tok_rows
    per_group = HQ // HK
    kv_width = HK * HD
    core = lax.axis_index("c")
    dp_size = lax.axis_size("dp")
    dp_index = lax.axis_index("dp")
    mine = jnp.stack([w_key, w_value])[core]
    arrived = [mine] + [
        lax.ppermute(mine, "dp", [(i, (i + by) % dp_size) for i in range(dp_size)])
        for by in range(1, dp_size)
    ]
    order = (dp_index - jnp.arange(dp_size, dtype=jnp.int32)) % dp_size
    mine_full = jnp.take(jnp.stack(arrived), order, axis=0).reshape(D, kv_width)
    other_full = lax.ppermute(mine_full, "c", [(0, 1), (1, 0)])
    first = core == 0
    key_full = jnp.where(first, mine_full, other_full)
    value_full = jnp.where(first, other_full, mine_full)
    key_own = jnp.dot(tokens, key_full, preferred_element_type=jnp.float32).astype(jnp.bfloat16)
    value_own = jnp.dot(tokens, value_full, preferred_element_type=jnp.float32).astype(jnp.bfloat16)
    kv_own = jnp.concatenate([key_own, value_own], axis=1)
    chips_back = distant // 2
    swap = [(0, 1), (1, 0)]
    fetched = [kv_own] + [from_behind(kv_own, CTX, 2 * back) for back in range(1, chips_back + 1)]
    partner_kv = lax.ppermute(jnp.stack(fetched), "c", swap)
    blocks = []
    for back in range(chips_back, 0, -1):
        blocks += [fetched[back], partner_kv[back - core]]
    window = jnp.concatenate(blocks + [kv_own], axis=0)
    device_index = lax.axis_index(CTX)
    first_row = device_index * tok_rows
    query_pos = first_row + jnp.arange(tok_rows, dtype=jnp.int32)
    key_pos = first_row - distant * tok_rows + jnp.arange((distant + 1) * tok_rows, dtype=jnp.int32)
    allowed = band_mask(
        query_pos, segment_of(lengths, query_pos), key_pos, segment_of(lengths, key_pos)
    )
    query_heads = queries.reshape(tok_rows, HK, per_group, HD)
    upstream_heads = upstream.reshape(tok_rows, HK, per_group, HD)
    scores = masked_scores(query_heads, window[:, :kv_width], allowed)
    highest, summed = score_stats(scores)
    log_total = highest + jnp.log(summed)
    softmax, soft_half = softmax_of(scores, log_total)
    mixed_half = values_of(soft_half, window[:, kv_width:]).astype(jnp.bfloat16)
    delta_sum = row_delta(upstream_heads, mixed_half)
    query_grad, kv_blocks = band_grads(
        softmax,
        soft_half,
        query_heads,
        upstream_heads,
        delta_sum,
        window[:, :kv_width],
        window[:, kv_width:],
        tok_rows,
    )
    crossed = jnp.stack(
        [kv_blocks[distant + 1 - 2 * back].astype(jnp.bfloat16) for back in range(1, chips_back + 1)]
    )
    from_partner = lax.ppermute(crossed, "c", swap).astype(jnp.float32)
    padded = jnp.concatenate([jnp.zeros_like(from_partner[:1]), from_partner, jnp.zeros_like(from_partner[:1])])
    own_grad = kv_blocks[distant] + padded[1 - core]
    for back in range(chips_back, 0, -1):
        mine_total = kv_blocks[distant - 2 * back] + padded[back + 1 - core]
        own_grad = own_grad + from_behind(
            mine_total.astype(jnp.bfloat16), CTX, -2 * back
        ).astype(jnp.float32)
    kv_grad = own_grad.astype(jnp.bfloat16)
    grad_input = (
        jnp.dot(kv_grad[:, :kv_width], key_full.T, preferred_element_type=jnp.float32)
        + jnp.dot(kv_grad[:, kv_width:], value_full.T, preferred_element_type=jnp.float32)
    ).astype(jnp.bfloat16)
    z_size, y_size, c_size = lax.axis_size("z"), lax.axis_size("y"), lax.axis_size("c")
    row_share = D // dp_size
    rows_z = row_share // z_size
    cols_cy = 2 * kv_width // (c_size * y_size)
    weight_part = jnp.einsum(
        "tazr,tcyj->cyazrj",
        tokens.reshape(tok_rows, dp_size, z_size, rows_z),
        kv_grad.reshape(tok_rows, c_size, y_size, cols_cy),
        preferred_element_type=jnp.float32,
    )
    partner = lax.ppermute(weight_part[1 - core].astype(jnp.bfloat16), "c", [(0, 1), (1, 0)])
    part = weight_part[core] + partner.astype(jnp.float32)
    part = lax.psum_scatter(part.astype(jnp.bfloat16), "y", scatter_dimension=0, tiled=True)[0]
    part, grad_input, query_grad = lax.optimization_barrier((part, grad_input, query_grad))
    part = part.astype(jnp.float32)
    step = 1
    while step < dp_size:
        bit = (dp_index // step) % 2
        split = part.reshape(part.shape[0] // 2, 2, *part.shape[1:])
        sent = lax.ppermute(
            split[:, 1 - bit].astype(jnp.bfloat16), "dp", [(i, i ^ step) for i in range(dp_size)]
        )
        part = split[:, bit] + sent.astype(jnp.float32)
        step *= 2
    part = part[0]
    step = 1
    while step < z_size:
        half = part.astype(jnp.bfloat16)
        part = half.astype(jnp.float32) + lax.ppermute(
            half, "z", [(i, i ^ step) for i in range(z_size)]
        ).astype(jnp.float32)
        step *= 2
    part = part.astype(jnp.bfloat16).reshape(row_share, cols_cy)
    part = lax.all_gather(part, "y", axis=0)
    part = lax.all_gather(part, "c", axis=0)
    weight_grad = jnp.transpose(part, (2, 0, 1, 3)).reshape(row_share, 2 * kv_width)
    attended = mixed_half.reshape(1, tok_rows, HQ * HD)
    grad_query = query_grad.astype(jnp.bfloat16).reshape(1, tok_rows, HQ * HD)
    return (
        attended,
        grad_query,
        grad_input.reshape(1, tok_rows, D),
        weight_grad[:, :kv_width],
        weight_grad[:, kv_width:],
    )


def solution(mesh):
    z_size = mesh.devices.shape[1] // 8
    split = jax.sharding.Mesh(
        mesh.devices.reshape(mesh.devices.shape[0], z_size, 4, 2), ("dp",) + CTX
    )
    tokens_spec = P("dp", CTX, None)
    in_specs = (tokens_spec, tokens_spec, P("dp", None), P("dp", None), P("dp", None), tokens_spec)
    out_specs = (tokens_spec, tokens_spec, tokens_spec, P("dp", None), P("dp", None))
    return jax.shard_map(shards, mesh=split, in_specs=in_specs, out_specs=out_specs, check_vma=False)
```

```python
import jax
import jax.numpy as jnp
from jax import lax
from jax.sharding import PartitionSpec as P

D = 2304
HQ = 4
HK = 2
HD = 256
WINDOW = 2048


FLOOR = -1e30
CTX = ("z", "y", "c")


def ctx_size():
    return lax.axis_size("z") * lax.axis_size("y") * lax.axis_size("c")


def from_behind(value, axis, by):
    peers = ctx_size()
    pairs = [(i, i + by) for i in range(peers) if 0 <= i + by < peers]
    return lax.ppermute(value, axis, pairs)


def segment_of(lengths, positions):
    doc_ends = jnp.cumsum(lengths, dtype=jnp.int32)
    return jnp.sum(
        (doc_ends[None, :] <= positions[:, None]).astype(jnp.int32), axis=1, dtype=jnp.int32
    )


def band_mask(query_pos, query_seg, key_pos, key_seg):
    distance_gap = query_pos[:, None] - key_pos[None, :]
    inside = (distance_gap >= 0) & (distance_gap < WINDOW) & (key_pos[None, :] >= 0)
    return inside & (query_seg[:, None] == key_seg[None, :])


def masked_scores(query_heads, key_rows, allowed):
    key_heads = key_rows.reshape(key_rows.shape[0], HK, HD)
    scores = jnp.einsum(
        "qkgd,tkd->kgqt", query_heads, key_heads, preferred_element_type=jnp.float32
    ) * HD ** (-0.5)
    return jnp.where(allowed[None, None], scores, -jnp.inf)


def score_stats(scores):
    highest = jnp.maximum(jnp.max(scores, axis=-1), FLOOR)
    summed = jnp.sum(jnp.exp(scores - highest[..., None]), axis=-1)
    return (highest, summed)


def softmax_of(scores, log_total):
    softmax = jnp.exp(scores - log_total[..., None])
    return (softmax, softmax.astype(jnp.bfloat16))


def values_of(soft_half, value_rows):
    value_heads = value_rows.reshape(value_rows.shape[0], HK, HD)
    return jnp.einsum("kgqt,tkd->qkgd", soft_half, value_heads, preferred_element_type=jnp.float32)


def row_delta(upstream_heads, mixed_half):
    products = upstream_heads.astype(jnp.float32) * mixed_half.astype(jnp.float32)
    return jnp.transpose(jnp.sum(products, axis=-1), (1, 2, 0))


def band_grads(softmax, soft_half, query_heads, upstream_heads, delta_sum, key_rows, value_rows, block_rows):
    span_rows = key_rows.shape[0]
    key_heads = key_rows.reshape(span_rows, HK, HD)
    value_heads = value_rows.reshape(span_rows, HK, HD)
    prob_grad = jnp.einsum(
        "qkgd,tkd->kgqt", upstream_heads, value_heads, preferred_element_type=jnp.float32
    )
    score_grad = (softmax * (prob_grad - delta_sum[..., None]) * HD ** (-0.5)).astype(jnp.bfloat16)
    kv_blocks = []
    for block in range(span_rows // block_rows):
        cols = slice(block * block_rows, (block + 1) * block_rows)
        key_grad = jnp.einsum(
            "kgqt,qkgd->tkd", score_grad[..., cols], query_heads, preferred_element_type=jnp.float32
        )
        value_grad = jnp.einsum(
            "kgqt,qkgd->tkd", soft_half[..., cols], upstream_heads, preferred_element_type=jnp.float32
        )
        kv_blocks.append(
            jnp.concatenate(
                [key_grad.reshape(block_rows, HK * HD), value_grad.reshape(block_rows, HK * HD)], axis=1
            )
        )
    query_grad = jnp.einsum(
        "kgqt,tkd->qkgd", score_grad, key_heads, preferred_element_type=jnp.float32
    )
    return (query_grad, kv_blocks)


def shards(inputs, query, w_key, w_value, doc_lengths, grad_out):
    tokens = inputs[0]
    queries = query[0]
    upstream = grad_out[0]
    lengths = doc_lengths[0]
    tok_rows = tokens.shape[0]
    distant = WINDOW // tok_rows
    per_group = HQ // HK
    kv_width = HK * HD
    core = lax.axis_index("c")
    dp_size = lax.axis_size("dp")
    dp_index = lax.axis_index("dp")
    mine = jnp.stack([w_key, w_value])[core]
    arrived = [mine] + [
        lax.ppermute(mine, "dp", [(i, (i + by) % dp_size) for i in range(dp_size)])
        for by in range(1, dp_size)
    ]
    order = (dp_index - jnp.arange(dp_size, dtype=jnp.int32)) % dp_size
    mine_full = jnp.take(jnp.stack(arrived), order, axis=0).reshape(D, kv_width)
    other_full = lax.ppermute(mine_full, "c", [(0, 1), (1, 0)])
    first = core == 0
    key_full = jnp.where(first, mine_full, other_full)
    value_full = jnp.where(first, other_full, mine_full)
    key_own = jnp.dot(tokens, key_full, preferred_element_type=jnp.float32).astype(jnp.bfloat16)
    value_own = jnp.dot(tokens, value_full, preferred_element_type=jnp.float32).astype(jnp.bfloat16)
    kv_own = jnp.concatenate([key_own, value_own], axis=1)
    chips_back = distant // 2
    swap = [(0, 1), (1, 0)]
    fetched = [kv_own] + [from_behind(kv_own, CTX, 2 * back) for back in range(1, chips_back + 1)]
    partner_kv = lax.ppermute(jnp.stack(fetched), "c", swap)
    blocks = []
    for back in range(chips_back, 0, -1):
        blocks += [fetched[back], partner_kv[back - core]]
    window = jnp.concatenate(blocks + [kv_own], axis=0)
    device_index = lax.axis_index(CTX)
    first_row = device_index * tok_rows
    query_pos = first_row + jnp.arange(tok_rows, dtype=jnp.int32)
    key_pos = first_row - distant * tok_rows + jnp.arange((distant + 1) * tok_rows, dtype=jnp.int32)
    allowed = band_mask(
        query_pos, segment_of(lengths, query_pos), key_pos, segment_of(lengths, key_pos)
    )
    query_heads = queries.reshape(tok_rows, HK, per_group, HD)
    upstream_heads = upstream.reshape(tok_rows, HK, per_group, HD)
    scores = masked_scores(query_heads, window[:, :kv_width], allowed)
    highest, summed = score_stats(scores)
    log_total = highest + jnp.log(summed)
    softmax, soft_half = softmax_of(scores, log_total)
    mixed_half = values_of(soft_half, window[:, kv_width:]).astype(jnp.bfloat16)
    delta_sum = row_delta(upstream_heads, mixed_half)
    query_grad, kv_blocks = band_grads(
        softmax,
        soft_half,
        query_heads,
        upstream_heads,
        delta_sum,
        window[:, :kv_width],
        window[:, kv_width:],
        tok_rows,
    )
    crossed = jnp.stack(
        [kv_blocks[distant + 1 - 2 * back].astype(jnp.bfloat16) for back in range(1, chips_back + 1)]
    )
    from_partner = lax.ppermute(crossed, "c", swap).astype(jnp.float32)
    padded = jnp.concatenate([jnp.zeros_like(from_partner[:1]), from_partner, jnp.zeros_like(from_partner[:1])])
    own_grad = kv_blocks[distant] + padded[1 - core]
    for back in range(chips_back, 0, -1):
        mine_total = kv_blocks[distant - 2 * back] + padded[back + 1 - core]
        own_grad = own_grad + from_behind(
            mine_total.astype(jnp.bfloat16), CTX, -2 * back
        ).astype(jnp.float32)
    kv_grad = own_grad.astype(jnp.bfloat16)
    grad_input = (
        jnp.dot(kv_grad[:, :kv_width], key_full.T, preferred_element_type=jnp.float32)
        + jnp.dot(kv_grad[:, kv_width:], value_full.T, preferred_element_type=jnp.float32)
    ).astype(jnp.bfloat16)
    z_size, y_size, c_size = lax.axis_size("z"), lax.axis_size("y"), lax.axis_size("c")
    row_share = D // dp_size
    rows_z = row_share // z_size
    cols_cy = 2 * kv_width // (c_size * y_size)
    weight_part = jnp.einsum(
        "tazr,tcyj->cyazrj",
        tokens.reshape(tok_rows, dp_size, z_size, rows_z),
        kv_grad.reshape(tok_rows, c_size, y_size, cols_cy),
        preferred_element_type=jnp.float32,
    )
    partner = lax.ppermute(weight_part[1 - core].astype(jnp.bfloat16), "c", [(0, 1), (1, 0)])
    part = weight_part[core] + partner.astype(jnp.float32)
    part = lax.psum_scatter(part.astype(jnp.bfloat16), "y", scatter_dimension=0, tiled=True)[0]
    part, grad_input, query_grad = lax.optimization_barrier((part, grad_input, query_grad))
    part = part.astype(jnp.float32)
    step = 1
    while step < dp_size:
        bit = (dp_index // step) % 2
        split = part.reshape(part.shape[0] // 2, 2, *part.shape[1:])
        sent = lax.ppermute(
            split[:, 1 - bit].astype(jnp.bfloat16), "dp", [(i, i ^ step) for i in range(dp_size)]
        )
        part = split[:, bit] + sent.astype(jnp.float32)
        step *= 2
    part = part[0]
    step = 1
    while step < z_size:
        half = part.astype(jnp.bfloat16)
        part = half.astype(jnp.float32) + lax.ppermute(
            half, "z", [(i, i ^ step) for i in range(z_size)]
        ).astype(jnp.float32)
        step *= 2
    part = part.astype(jnp.bfloat16).reshape(row_share, cols_cy)
    part = lax.all_gather(part, "y", axis=0)
    mate = lax.ppermute(part, "c", swap)
    part = jnp.where(core == 0, jnp.stack([part, mate]), jnp.stack([mate, part]))
    weight_grad = jnp.transpose(part, (2, 0, 1, 3)).reshape(row_share, 2 * kv_width)
    attended = mixed_half.reshape(1, tok_rows, HQ * HD)
    grad_query = query_grad.astype(jnp.bfloat16).reshape(1, tok_rows, HQ * HD)
    return (
        attended,
        grad_query,
        grad_input.reshape(1, tok_rows, D),
        weight_grad[:, :kv_width],
        weight_grad[:, kv_width:],
    )


def solution(mesh):
    z_size = mesh.devices.shape[1] // 8
    split = jax.sharding.Mesh(
        mesh.devices.reshape(mesh.devices.shape[0], z_size, 4, 2), ("dp",) + CTX
    )
    tokens_spec = P("dp", CTX, None)
    in_specs = (tokens_spec, tokens_spec, P("dp", None), P("dp", None), P("dp", None), tokens_spec)
    out_specs = (tokens_spec, tokens_spec, tokens_spec, P("dp", None), P("dp", None))
    return jax.shard_map(shards, mesh=split, in_specs=in_specs, out_specs=out_specs, check_vma=False)
```

```python
import jax
import jax.numpy as jnp
from jax import lax
from jax.sharding import PartitionSpec as P

D = 2304
HQ = 4
HK = 2
HD = 256
WINDOW = 2048


FLOOR = -1e30
CTX = ("z", "y", "c")


def ctx_size():
    return lax.axis_size("z") * lax.axis_size("y") * lax.axis_size("c")


def from_behind(value, axis, by):
    peers = ctx_size()
    pairs = [(i, i + by) for i in range(peers) if 0 <= i + by < peers]
    return lax.ppermute(value, axis, pairs)


def segment_of(lengths, positions):
    doc_ends = jnp.cumsum(lengths, dtype=jnp.int32)
    return jnp.sum(
        (doc_ends[None, :] <= positions[:, None]).astype(jnp.int32), axis=1, dtype=jnp.int32
    )


def band_mask(query_pos, query_seg, key_pos, key_seg):
    distance_gap = query_pos[:, None] - key_pos[None, :]
    inside = (distance_gap >= 0) & (distance_gap < WINDOW) & (key_pos[None, :] >= 0)
    return inside & (query_seg[:, None] == key_seg[None, :])


def masked_scores(query_heads, key_rows, allowed):
    key_heads = key_rows.reshape(key_rows.shape[0], HK, HD)
    scores = jnp.einsum(
        "qkgd,tkd->kgqt", query_heads, key_heads, preferred_element_type=jnp.float32
    ) * HD ** (-0.5)
    return jnp.where(allowed[None, None], scores, -jnp.inf)


def score_stats(scores):
    highest = jnp.maximum(jnp.max(scores, axis=-1), FLOOR)
    summed = jnp.sum(jnp.exp(scores - highest[..., None]), axis=-1)
    return (highest, summed)


def softmax_of(scores, log_total):
    softmax = jnp.exp(scores - log_total[..., None])
    return (softmax, softmax.astype(jnp.bfloat16))


def values_of(soft_half, value_rows):
    value_heads = value_rows.reshape(value_rows.shape[0], HK, HD)
    return jnp.einsum("kgqt,tkd->qkgd", soft_half, value_heads, preferred_element_type=jnp.float32)


def row_delta(upstream_heads, mixed_half):
    products = upstream_heads.astype(jnp.float32) * mixed_half.astype(jnp.float32)
    return jnp.transpose(jnp.sum(products, axis=-1), (1, 2, 0))


def band_grads(softmax, soft_half, query_heads, upstream_heads, delta_sum, key_rows, value_rows, block_rows):
    span_rows = key_rows.shape[0]
    key_heads = key_rows.reshape(span_rows, HK, HD)
    value_heads = value_rows.reshape(span_rows, HK, HD)
    prob_grad = jnp.einsum(
        "qkgd,tkd->kgqt", upstream_heads, value_heads, preferred_element_type=jnp.float32
    )
    score_grad = (softmax * (prob_grad - delta_sum[..., None]) * HD ** (-0.5)).astype(jnp.bfloat16)
    key_grad = jnp.einsum(
        "kgqt,qkgd->tkd", score_grad, query_heads, preferred_element_type=jnp.float32
    )
    value_grad = jnp.einsum(
        "kgqt,qkgd->tkd", soft_half, upstream_heads, preferred_element_type=jnp.float32
    )
    kv_all = jnp.concatenate(
        [key_grad.reshape(span_rows, HK * HD), value_grad.reshape(span_rows, HK * HD)], axis=1
    )
    kv_blocks = [
        kv_all[block * block_rows : (block + 1) * block_rows]
        for block in range(span_rows // block_rows)
    ]
    query_grad = jnp.einsum(
        "kgqt,tkd->qkgd", score_grad, key_heads, preferred_element_type=jnp.float32
    )
    return (query_grad, kv_blocks)


def shards(inputs, query, w_key, w_value, doc_lengths, grad_out):
    tokens = inputs[0]
    queries = query[0]
    upstream = grad_out[0]
    lengths = doc_lengths[0]
    tok_rows = tokens.shape[0]
    distant = WINDOW // tok_rows
    per_group = HQ // HK
    kv_width = HK * HD
    core = lax.axis_index("c")
    dp_size = lax.axis_size("dp")
    dp_index = lax.axis_index("dp")
    mine = jnp.stack([w_key, w_value])[core]
    arrived = [mine] + [
        lax.ppermute(mine, "dp", [(i, (i + by) % dp_size) for i in range(dp_size)])
        for by in range(1, dp_size)
    ]
    reverse = jnp.stack([arrived[0]] + arrived[:0:-1])
    mine_full = jnp.roll(reverse, dp_index, axis=0).reshape(D, kv_width)
    other_full = lax.ppermute(mine_full, "c", [(0, 1), (1, 0)])
    first = core == 0
    key_full = jnp.where(first, mine_full, other_full)
    value_full = jnp.where(first, other_full, mine_full)
    key_own = jnp.dot(tokens, key_full, preferred_element_type=jnp.float32).astype(jnp.bfloat16)
    value_own = jnp.dot(tokens, value_full, preferred_element_type=jnp.float32).astype(jnp.bfloat16)
    kv_own = jnp.concatenate([key_own, value_own], axis=1)
    chips_back = distant // 2
    swap = [(0, 1), (1, 0)]
    fetched = [kv_own] + [from_behind(kv_own, CTX, 2 * back) for back in range(1, chips_back + 1)]
    partner_kv = lax.ppermute(jnp.stack(fetched), "c", swap)
    blocks = []
    for back in range(chips_back, 0, -1):
        blocks += [fetched[back], partner_kv[back - core]]
    window = jnp.concatenate(blocks + [kv_own], axis=0)
    device_index = lax.axis_index(CTX)
    first_row = device_index * tok_rows
    query_pos = first_row + jnp.arange(tok_rows, dtype=jnp.int32)
    key_pos = first_row - distant * tok_rows + jnp.arange((distant + 1) * tok_rows, dtype=jnp.int32)
    allowed = band_mask(
        query_pos, segment_of(lengths, query_pos), key_pos, segment_of(lengths, key_pos)
    )
    query_heads = queries.reshape(tok_rows, HK, per_group, HD)
    upstream_heads = upstream.reshape(tok_rows, HK, per_group, HD)
    scores = masked_scores(query_heads, window[:, :kv_width], allowed)
    highest, summed = score_stats(scores)
    log_total = highest + jnp.log(summed)
    softmax, soft_half = softmax_of(scores, log_total)
    mixed_half = values_of(soft_half, window[:, kv_width:]).astype(jnp.bfloat16)
    delta_sum = row_delta(upstream_heads, mixed_half)
    query_grad, kv_blocks = band_grads(
        softmax,
        soft_half,
        query_heads,
        upstream_heads,
        delta_sum,
        window[:, :kv_width],
        window[:, kv_width:],
        tok_rows,
    )
    crossed = jnp.stack(
        [kv_blocks[distant + 1 - 2 * back].astype(jnp.bfloat16) for back in range(1, chips_back + 1)]
    )
    from_partner = lax.ppermute(crossed, "c", swap).astype(jnp.float32)
    padded = jnp.concatenate([jnp.zeros_like(from_partner[:1]), from_partner, jnp.zeros_like(from_partner[:1])])
    own_grad = kv_blocks[distant] + padded[1 - core]
    for back in range(chips_back, 0, -1):
        mine_total = kv_blocks[distant - 2 * back] + padded[back + 1 - core]
        own_grad = own_grad + from_behind(
            mine_total.astype(jnp.bfloat16), CTX, -2 * back
        ).astype(jnp.float32)
    kv_grad = own_grad.astype(jnp.bfloat16)
    grad_input = (
        jnp.dot(kv_grad[:, :kv_width], key_full.T, preferred_element_type=jnp.float32)
        + jnp.dot(kv_grad[:, kv_width:], value_full.T, preferred_element_type=jnp.float32)
    ).astype(jnp.bfloat16)
    z_size, y_size, c_size = lax.axis_size("z"), lax.axis_size("y"), lax.axis_size("c")
    row_share = D // dp_size
    rows_z = row_share // z_size
    cols_cy = 2 * kv_width // (c_size * y_size)
    weight_part = jnp.einsum(
        "tazr,tcyj->cyazrj",
        tokens.reshape(tok_rows, dp_size, z_size, rows_z),
        kv_grad.reshape(tok_rows, c_size, y_size, cols_cy),
        preferred_element_type=jnp.float32,
    )
    partner = lax.ppermute(weight_part[1 - core].astype(jnp.bfloat16), "c", [(0, 1), (1, 0)])
    part = weight_part[core] + partner.astype(jnp.float32)
    part = lax.psum_scatter(part.astype(jnp.bfloat16), "y", scatter_dimension=0, tiled=True)[0]
    part, grad_input, query_grad = lax.optimization_barrier((part, grad_input, query_grad))
    part = part.astype(jnp.float32)
    step = 1
    while step < dp_size:
        bit = (dp_index // step) % 2
        split = part.reshape(part.shape[0] // 2, 2, *part.shape[1:])
        sent = lax.ppermute(
            split[:, 1 - bit].astype(jnp.bfloat16), "dp", [(i, i ^ step) for i in range(dp_size)]
        )
        part = split[:, bit] + sent.astype(jnp.float32)
        step *= 2
    part = part[0]
    step = 1
    while step < z_size:
        half = part.astype(jnp.bfloat16)
        part = half.astype(jnp.float32) + lax.ppermute(
            half, "z", [(i, i ^ step) for i in range(z_size)]
        ).astype(jnp.float32)
        step *= 2
    part = part.astype(jnp.bfloat16).reshape(row_share, cols_cy)
    part = lax.all_gather(part, "y", axis=0)
    mate = lax.ppermute(part, "c", swap)
    part = jnp.where(core == 0, jnp.stack([part, mate]), jnp.stack([mate, part]))
    weight_grad = jnp.transpose(part, (2, 0, 1, 3)).reshape(row_share, 2 * kv_width)
    attended = mixed_half.reshape(1, tok_rows, HQ * HD)
    grad_query = query_grad.astype(jnp.bfloat16).reshape(1, tok_rows, HQ * HD)
    return (
        attended,
        grad_query,
        grad_input.reshape(1, tok_rows, D),
        weight_grad[:, :kv_width],
        weight_grad[:, kv_width:],
    )


def solution(mesh):
    z_size = mesh.devices.shape[1] // 8
    split = jax.sharding.Mesh(
        mesh.devices.reshape(mesh.devices.shape[0], z_size, 4, 2), ("dp",) + CTX
    )
    tokens_spec = P("dp", CTX, None)
    in_specs = (tokens_spec, tokens_spec, P("dp", None), P("dp", None), P("dp", None), tokens_spec)
    out_specs = (tokens_spec, tokens_spec, tokens_spec, P("dp", None), P("dp", None))
    return jax.shard_map(shards, mesh=split, in_specs=in_specs, out_specs=out_specs, check_vma=False)
```
